128 devices in a mesh: prow: 4 (over y), pcol: 32 (over z, x, core).
Axes of the slice: x: 4, y: 4, z: 4, core: 2. Of those that a mesh axis runs over, the one named last changes fastest.
Arguments:
- diag_blocks: float32 [2, 64, 64], P(None, 'prow')
- panel_rows: float32 [2, 64, 8192], P(None, None, ('prow', 'pcol')), may hold values from -18 to 18
- child_map: int32 [2, 128], replicated, may hold values from 0 to 255, as said below
- front: float32 [16384, 16384], P('prow', 'pcol'), may hold values from -6 to 6
Outputs:
- updated_front: float32 [16384, 16384], P('prow', 'pcol')
The draws below stay inside these ranges and needn't reach their ends.
Inputs may be any that keep to these rules, and one draw needn't show every extreme that they name: `child_map`: for each panel and each g below 4, the child blocks 32 * g to 32 * g + 31 map, in rising order, to distinct block rows from g * 64 to g * 64 + 63, the first and the last of these always among them.
All inputs are finite; a program needn't handle non-finite values.
Results may differ from the reference program's by a relative error of at most 0.0003.
Values sent between devices are 32-bit elements; how exact they have to be, the bound alone decides.
No kernel may reach another device: no remote copies, remote signals or barrier semaphores. Data moves between devices by JAX's collectives and lax.ppermute only.
A program may use at most 64 MiB of HBM per device.

```python
import jax
import jax.numpy as jnp
from jax import lax

B = 64
PCOLB = 8
NF = 16384
CHILD = 128
N_PROW = 4
N_PCOL = 32


def draw_diag_blocks(key, part):
    first_key, second_key = jax.random.split(key)
    noise = jax.random.uniform(first_key, (2, B, B), jnp.float32, -1.0, 1.0)
    symmetric = 0.5 * (noise + jnp.swapaxes(noise, 1, 2))
    boost = jax.random.uniform(second_key, (2, B), jnp.float32, 1.0, 2.0)
    identity = jnp.eye(B, dtype=jnp.float32)
    return symmetric * (1.0 - identity) + identity[None, :, :] * (B * boost)[:, :, None]


def draw_child_map(key, part):
    row_blocks = PCOLB * N_PCOL // N_PROW
    key_list = jax.random.split(key, 2 * N_PROW)

    def choose_rows(sub_key):
        middle = jax.random.permutation(sub_key, row_blocks - 2)[:N_PCOL - 2].astype(jnp.int32) + 1
        ends = jnp.array([0, row_blocks - 1], dtype=jnp.int32)
        return jnp.sort(jnp.concatenate([ends, middle]))
    chosen = jax.vmap(choose_rows)(key_list).reshape(2, N_PROW, N_PCOL)
    offsets = (jnp.arange(N_PROW, dtype=jnp.int32) * row_blocks)[None, :, None]
    return (chosen + offsets).reshape(2, N_PROW * N_PCOL).astype(jnp.int32)


def level_of(own_key, shape, cuts, least, top_value):
    def one(position, shards_of):
        heights = jax.random.uniform(jax.random.fold_in(jax.random.fold_in(own_key, 6), position), (shards_of,), jnp.float32, least / len(cuts), top_value / len(cuts))
        return jnp.repeat(jnp.exp(heights), shape[position] // shards_of).reshape((-1,) + (1,) * (len(shape) - position - 1))

    gain = one(*cuts[0])
    for cut in cuts[1:]:
        gain = gain * one(*cut)
    return gain


def normal_values(rng, dims, scale, reach, cuts=(), held_as=jnp.bfloat16):
    values = jax.random.normal(rng, dims, jnp.float32) * scale
    if len(cuts) > 0:
        values = level_of(rng, dims, cuts, -0.22, 0.18) * values
    return jnp.clip(values, min=-reach, max=reach).astype(held_as)


def setup_inputs(seed: int = 0) -> dict:
    keys = jax.random.split(jax.random.key(seed), 5)
    return {
        "diag_blocks": draw_diag_blocks(jax.random.fold_in(keys[4], 71), 0),
        "panel_rows": normal_values(keys[1], (2, B, CHILD * B), 3.0, 18.0, ((2, 128),), jnp.float32),
        "child_map": draw_child_map(jax.random.fold_in(keys[4], 71), 0),
        "front": normal_values(keys[3], (NF, NF), 1.0, 6.0, ((0, 4), (1, 32)), jnp.float32),
    }


def expand_all(factored, panel_map, block_total):
    width = factored.shape[0]
    columns = (panel_map[:, None] * width + jnp.arange(width, dtype=jnp.int32)[None, :]).reshape(-1)
    return jnp.zeros((width, block_total * width), jnp.float32).at[:, columns].set(factored)

def reference(diag_blocks, panel_rows, child_map, front):
    block_total = PCOLB * N_PCOL
    order = block_total * B
    pieces = []
    for panel in range(2):
        lower_factor = jnp.linalg.cholesky(diag_blocks[panel])
        factored = lax.linalg.triangular_solve(lower_factor, panel_rows[panel], left_side=True, lower=True)
        pieces.append(expand_all(factored, child_map[panel], block_total))
    stacked = jnp.concatenate(pieces, axis=0)
    column_block = jnp.arange(order, dtype=jnp.int32) // B

    def one_strip(index):
        strip = lax.dynamic_slice_in_dim(stacked, index * B, B, 1)
        update = lax.dot_general(strip.astype(jnp.float32), stacked.astype(jnp.float32), (((0,), (0,)), ((), ())), precision=lax.Precision.HIGHEST, preferred_element_type=jnp.float32)
        front_rows = lax.dynamic_slice_in_dim(front, index * B, B, 0)
        return front_rows - jnp.where(index >= column_block[None, :], update, 0.0)
    strips = lax.map(one_strip, jnp.arange(block_total, dtype=jnp.int32))
    return strips.reshape(order, order)
```

```python
import functools

import jax
import jax.numpy as jnp
from jax import lax
from jax.experimental import pallas as pl
from jax.experimental.pallas import tpu as pltpu
from jax.sharding import PartitionSpec as P

HIGHEST = lax.Precision.HIGHEST
TILE_ROWS = 512


def front_kernel(width, row_blocks, col_blocks, table_ref, place_ref,
                 group_ref, right_ref, front_ref, out_ref, left_ref):
    step = pl.program_id(0)
    tile_rows, cols = front_ref.shape
    per_tile = tile_rows // width
    lane = lax.broadcasted_iota(jnp.int32, (width, 2 * width), 1)
    for local in range(per_tile):
        block = step * per_tile + local
        first = table_ref[0, block]
        second = table_ref[1, block]
        from_first = group_ref[jnp.maximum(first, 0)]
        from_second = group_ref[jnp.maximum(second, 0)]
        left_ref[local * width:(local + 1) * width, :] = jnp.where(
            lane < width,
            jnp.where(first >= 0, from_first, 0.0),
            jnp.where(second >= 0, from_second, 0.0),
        )
    update = jnp.dot(left_ref[...], right_ref[...], precision=HIGHEST,
                     preferred_element_type=jnp.float32)
    row0 = place_ref[0] * (row_blocks * width) + step * tile_rows
    col0 = place_ref[1] * (col_blocks * width)
    rows = row0 + lax.broadcasted_iota(jnp.int32, (tile_rows, cols), 0)
    cols_at = col0 + lax.broadcasted_iota(jnp.int32, (tile_rows, cols), 1)
    lower = rows >= jnp.bitwise_and(cols_at, -width)
    out_ref[...] = front_ref[...] - jnp.where(lower, update, 0.0)


def apply_update(table, place, group, right, front, width, row_blocks, col_blocks):
    rows, cols = front.shape
    tiles = rows // TILE_ROWS
    kernel = functools.partial(front_kernel, width, row_blocks, col_blocks)
    return pl.pallas_call(
        kernel,
        out_shape=jax.ShapeDtypeStruct(front.shape, front.dtype),
        grid_spec=pltpu.PrefetchScalarGridSpec(
            num_scalar_prefetch=2,
            grid=(tiles,),
            in_specs=[
                pl.BlockSpec(group.shape, lambda i, t, p: (0, 0, 0)),
                pl.BlockSpec(right.shape, lambda i, t, p: (0, 0)),
                pl.BlockSpec((TILE_ROWS, cols), lambda i, t, p: (i, 0)),
            ],
            out_specs=pl.BlockSpec((TILE_ROWS, cols), lambda i, t, p: (i, 0)),
            scratch_shapes=[pltpu.VMEM((TILE_ROWS, 2 * width), jnp.float32)],
        ),
        cost_estimate=pl.CostEstimate(
            flops=2 * rows * cols * 2 * width,
            bytes_accessed=2 * rows * cols * 4 + group.size * 4 + right.size * 4,
            transcendentals=0,
        ),
    )(table, place, group, right, front)


def first_match(mapping, targets):
    hit = mapping[:, :, None] == targets[None, None, :]
    index = jnp.argmax(hit, axis=1).astype(jnp.int32)
    return jnp.where(jnp.any(hit, axis=1), index, -1)


def per_device(diag_blocks, panel_rows, child_map, front):
    width = panel_rows.shape[1]
    row_index = lax.axis_index("prow")
    col_index = lax.axis_index("pcol")
    col_count = lax.axis_size("pcol")
    row_blocks = front.shape[0] // width
    col_blocks = front.shape[1] // width

    local = jnp.transpose(panel_rows, (2, 0, 1)).reshape(width, 2 * width)
    group = lax.all_gather(local, "pcol", axis=0)

    whole_diag = lax.all_gather(diag_blocks, "prow", axis=1, tiled=True)
    lower_factor = jnp.linalg.cholesky(whole_diag)
    eye = jnp.broadcast_to(jnp.eye(width, dtype=jnp.float32), whole_diag.shape)
    inverse_factor = lax.linalg.triangular_solve(
        lower_factor, eye, left_side=True, lower=True)
    inverse = jnp.einsum("pca,pcb->pab", inverse_factor, inverse_factor,
                         precision=HIGHEST)

    own_map = lax.dynamic_slice_in_dim(child_map, row_index * col_count, col_count, 1)
    table = first_match(own_map - row_index * row_blocks,
                        jnp.arange(row_blocks, dtype=jnp.int32))

    first_col = col_index * col_blocks
    source = first_col // row_blocks
    source_map = lax.dynamic_slice_in_dim(child_map, source * col_count, col_count, 1)
    picks = first_match(source_map, first_col + jnp.arange(col_blocks, dtype=jnp.int32))
    keep = (picks >= 0) & (row_index == source)
    select = (picks[:, :, None] == jnp.arange(col_count, dtype=jnp.int32)) & keep[:, :, None]
    window = jnp.einsum("pjk,kbpa->pjba", select.astype(jnp.float32),
                        group.reshape(col_count, width, 2, width), precision=HIGHEST)
    window = lax.psum(window, "prow")
    right = jnp.einsum("pxa,pjba->pxjb", inverse, window, precision=HIGHEST)
    right = right.reshape(2 * width, col_blocks * width)

    place = jnp.stack([row_index, col_index]).astype(jnp.int32)
    return apply_update(table, place, group, right, front, width, row_blocks, col_blocks)


def solution(mesh):
    return jax.shard_map(
        per_device,
        mesh=mesh,
        in_specs=(P(None, "prow", None), P(None, None, ("prow", "pcol")), P(), P("prow", "pcol")),
        out_specs=P("prow", "pcol"),
        check_vma=False,
    )
```

```python
import functools

import jax
import numpy as np
import jax.numpy as jnp
from jax import lax
from jax.experimental import pallas as pl
from jax.experimental.pallas import tpu as pltpu
from jax.sharding import PartitionSpec as P

HIGHEST = lax.Precision.HIGHEST
TILE_ROWS = 512


def split_bf16(value):
    scaled = value * 65537.0
    high = scaled - (scaled - value)
    return high.astype(jnp.bfloat16), (value - high).astype(jnp.bfloat16)


def front_kernel(width, row_blocks, col_blocks, table_ref, place_ref,
                 group_ref, high_ref, low_ref, front_ref, out_ref, left_ref):
    step = pl.program_id(0)
    tile_rows, cols = front_ref.shape
    per_tile = tile_rows // width
    lane = lax.broadcasted_iota(jnp.int32, (width, 2 * width), 1)
    for local in range(per_tile):
        block = step * per_tile + local
        first = table_ref[0, block]
        second = table_ref[1, block]
        from_first = group_ref[jnp.maximum(first, 0)]
        from_second = group_ref[jnp.maximum(second, 0)]
        left_ref[local * width:(local + 1) * width, :] = jnp.where(
            lane < width,
            jnp.where(first >= 0, from_first, 0.0),
            jnp.where(second >= 0, from_second, 0.0),
        )
    left_high, left_low = split_bf16(left_ref[...])
    right_high = high_ref[...]
    update = jnp.dot(left_high, right_high, preferred_element_type=jnp.float32)
    update += jnp.dot(left_high, low_ref[...], preferred_element_type=jnp.float32)
    update += jnp.dot(left_low, right_high, preferred_element_type=jnp.float32)
    row0 = place_ref[0] * (row_blocks * width) + step * tile_rows
    col0 = place_ref[1] * (col_blocks * width)
    rows = row0 + lax.broadcasted_iota(jnp.int32, (tile_rows, cols), 0)
    cols_at = col0 + lax.broadcasted_iota(jnp.int32, (tile_rows, cols), 1)
    lower = rows >= jnp.bitwise_and(cols_at, -width)
    out_ref[...] = front_ref[...] - jnp.where(lower, update, 0.0)


def apply_update(table, place, group, right, front, width, row_blocks, col_blocks):
    rows, cols = front.shape
    high, low = split_bf16(right)
    tiles = rows // TILE_ROWS
    kernel = functools.partial(front_kernel, width, row_blocks, col_blocks)
    return pl.pallas_call(
        kernel,
        out_shape=jax.ShapeDtypeStruct(front.shape, front.dtype),
        grid_spec=pltpu.PrefetchScalarGridSpec(
            num_scalar_prefetch=2,
            grid=(tiles,),
            in_specs=[
                pl.BlockSpec(group.shape, lambda i, t, p: (0, 0, 0)),
                pl.BlockSpec(right.shape, lambda i, t, p: (0, 0)),
                pl.BlockSpec(right.shape, lambda i, t, p: (0, 0)),
                pl.BlockSpec((TILE_ROWS, cols), lambda i, t, p: (i, 0)),
            ],
            out_specs=pl.BlockSpec((TILE_ROWS, cols), lambda i, t, p: (i, 0)),
            scratch_shapes=[pltpu.VMEM((TILE_ROWS, 2 * width), jnp.float32)],
        ),
        cost_estimate=pl.CostEstimate(
            flops=3 * 2 * rows * cols * 2 * width,
            bytes_accessed=2 * rows * cols * 4 + group.size * 4 + right.size * 4,
            transcendentals=0,
        ),
    )(table, place, group, high, low, front)


def doubling_gather(block, axis, count):
    bits = count.bit_length() - 1
    spread = [0]
    for bit in reversed(range(bits)):
        mask = 1 << bit
        other = lax.ppermute(block, axis, [(i, i ^ mask) for i in range(count)])
        block = jnp.concatenate([block, other], axis=0)
        spread = spread + [s ^ mask for s in spread]
    return block, spread


def first_match(mapping, targets):
    hit = mapping[:, :, None] == targets[None, None, :]
    index = jnp.argmax(hit, axis=1).astype(jnp.int32)
    return jnp.where(jnp.any(hit, axis=1), index, -1)


def per_device(diag_blocks, panel_rows, child_map, front):
    width = panel_rows.shape[1]
    row_index = lax.axis_index("prow")
    col_index = lax.axis_index("pcol")
    col_count = lax.axis_size("pcol")
    row_blocks = front.shape[0] // width
    col_blocks = front.shape[1] // width

    row_count = lax.axis_size("prow")

    local = jnp.transpose(panel_rows, (2, 0, 1)).reshape(width, 2 * width)
    group, spread = doubling_gather(local[None], "pcol", col_count)
    child_at = jnp.bitwise_xor(col_index, jnp.asarray(spread, jnp.int32))
    slot_of = jnp.bitwise_xor(col_index, jnp.arange(col_count, dtype=jnp.int32))
    slot_of = jnp.take(jnp.asarray(np.argsort(spread), jnp.int32), slot_of)

    pieces = [diag_blocks] + [
        lax.ppermute(diag_blocks, "prow", [(i, (i + k) % row_count) for i in range(row_count)])
        for k in range(1, row_count)
    ]
    order = (row_index - jnp.arange(row_count, dtype=jnp.int32)) % row_count
    whole_diag = sum(
        jnp.where((order == k)[None, :, None, None], piece[:, None], 0.0)
        for k, piece in enumerate(pieces)
    ).reshape(diag_blocks.shape[0], -1, diag_blocks.shape[2])
    lower_factor = jnp.linalg.cholesky(whole_diag)
    eye = jnp.broadcast_to(jnp.eye(width, dtype=jnp.float32), whole_diag.shape)
    inverse_factor = lax.linalg.triangular_solve(
        lower_factor, eye, left_side=True, lower=True)
    inverse = jnp.einsum("pca,pcb->pab", inverse_factor, inverse_factor,
                         precision=HIGHEST)

    own_map = lax.dynamic_slice_in_dim(child_map, row_index * col_count, col_count, 1)
    table = first_match(own_map - row_index * row_blocks,
                        jnp.arange(row_blocks, dtype=jnp.int32))
    table = jnp.where(table >= 0, jnp.take(slot_of, jnp.maximum(table, 0)), -1)

    first_col = col_index * col_blocks
    source = first_col // row_blocks
    source_map = lax.dynamic_slice_in_dim(child_map, source * col_count, col_count, 1)
    picks = first_match(source_map, first_col + jnp.arange(col_blocks, dtype=jnp.int32))
    keep = (picks >= 0) & (row_index == source)
    select = (picks[:, :, None] == child_at) & keep[:, :, None]
    window = jnp.einsum("pjk,kbpa->pjba", select.astype(jnp.float32),
                        group.reshape(col_count, width, 2, width), precision=HIGHEST)
    owner = [(c * col_blocks) // row_blocks for c in range(col_count)]
    window = window + sum(
        lax.ppermute(window, ("prow", "pcol"), [
            (owner[c] * col_count + c, (owner[c] + k) * col_count + c)
            for c in range(col_count) if owner[c] + k < row_count
        ])
        for k in range(1, row_count)
    )
    right = jnp.einsum("pxa,pjba->pxjb", inverse, window, precision=HIGHEST)
    right = right.reshape(2 * width, col_blocks * width)

    place = jnp.stack([row_index, col_index]).astype(jnp.int32)
    return apply_update(table, place, group, right, front, width, row_blocks, col_blocks)


def solution(mesh):
    return jax.shard_map(
        per_device,
        mesh=mesh,
        in_specs=(P(None, "prow", None), P(None, None, ("prow", "pcol")), P(), P("prow", "pcol")),
        out_specs=P("prow", "pcol"),
        check_vma=False,
    )
```

```python
import functools

import jax
import numpy as np
import jax.numpy as jnp
from jax import lax
from jax.experimental import pallas as pl
from jax.experimental.pallas import tpu as pltpu
from jax.sharding import PartitionSpec as P

HIGHEST = lax.Precision.HIGHEST
TILE_ROWS = 512


def split_bf16(value):
    scaled = value * 65537.0
    high = scaled - (scaled - value)
    return high.astype(jnp.bfloat16), (value - high).astype(jnp.bfloat16)


def front_kernel(width, row_blocks, col_blocks, table_ref, place_ref,
                 group_ref, high_ref, low_ref, front_ref, out_ref, left_ref):
    step = pl.program_id(0)
    tile_rows, cols = front_ref.shape
    per_tile = tile_rows // width
    lane = lax.broadcasted_iota(jnp.int32, (width, 2 * width), 1)
    for local in range(per_tile):
        block = step * per_tile + local
        first = table_ref[0, block]
        second = table_ref[1, block]
        from_first = group_ref[jnp.maximum(first, 0)]
        from_second = group_ref[jnp.maximum(second, 0)]
        left_ref[local * width:(local + 1) * width, :] = jnp.where(
            lane < width,
            jnp.where(first >= 0, from_first, 0.0),
            jnp.where(second >= 0, from_second, 0.0),
        )
    left_high, left_low = split_bf16(left_ref[...])
    right_high = high_ref[...]
    update = jnp.dot(left_high, right_high, preferred_element_type=jnp.float32)
    update += jnp.dot(left_high, low_ref[...], preferred_element_type=jnp.float32)
    update += jnp.dot(left_low, right_high, preferred_element_type=jnp.float32)
    row0 = place_ref[0] * (row_blocks * width) + step * tile_rows
    col0 = place_ref[1] * (col_blocks * width)
    rows = row0 + lax.broadcasted_iota(jnp.int32, (tile_rows, cols), 0)
    cols_at = col0 + lax.broadcasted_iota(jnp.int32, (tile_rows, cols), 1)
    lower = rows >= jnp.bitwise_and(cols_at, -width)
    out_ref[...] = front_ref[...] - jnp.where(lower, update, 0.0)


def apply_update(table, place, group, right, front, width, row_blocks, col_blocks):
    rows, cols = front.shape
    high, low = split_bf16(right)
    tiles = rows // TILE_ROWS
    kernel = functools.partial(front_kernel, width, row_blocks, col_blocks)
    return pl.pallas_call(
        kernel,
        out_shape=jax.ShapeDtypeStruct(front.shape, front.dtype),
        grid_spec=pltpu.PrefetchScalarGridSpec(
            num_scalar_prefetch=2,
            grid=(tiles,),
            in_specs=[
                pl.BlockSpec(group.shape, lambda i, t, p: (0, 0, 0)),
                pl.BlockSpec(right.shape, lambda i, t, p: (0, 0)),
                pl.BlockSpec(right.shape, lambda i, t, p: (0, 0)),
                pl.BlockSpec((TILE_ROWS, cols), lambda i, t, p: (i, 0)),
            ],
            out_specs=pl.BlockSpec((TILE_ROWS, cols), lambda i, t, p: (i, 0)),
            scratch_shapes=[pltpu.VMEM((TILE_ROWS, 2 * width), jnp.float32)],
        ),
        cost_estimate=pl.CostEstimate(
            flops=3 * 2 * rows * cols * 2 * width,
            bytes_accessed=2 * rows * cols * 4 + group.size * 4 + right.size * 4,
            transcendentals=0,
        ),
    )(table, place, group, high, low, front)


def doubling_gather(block, axis, count):
    bits = count.bit_length() - 1
    spread = [0]
    for bit in reversed(range(bits)):
        mask = 1 << bit
        other = lax.ppermute(block, axis, [(i, i ^ mask) for i in range(count)])
        block = jnp.concatenate([block, other], axis=0)
        spread = spread + [s ^ mask for s in spread]
    return block, spread


def first_match(mapping, targets):
    hit = mapping[:, :, None] == targets[None, None, :]
    index = jnp.argmax(hit, axis=1).astype(jnp.int32)
    return jnp.where(jnp.any(hit, axis=1), index, -1)


def per_device(diag_blocks, panel_rows, child_map, front):
    width = panel_rows.shape[1]
    row_index = lax.axis_index("prow")
    col_index = lax.axis_index("pcol")
    col_count = lax.axis_size("pcol")
    row_blocks = front.shape[0] // width
    col_blocks = front.shape[1] // width

    row_count = lax.axis_size("prow")

    local = jnp.transpose(panel_rows, (2, 0, 1)).reshape(width, 2 * width)
    group, spread = doubling_gather(local[None], "pcol", col_count)
    child_at = jnp.bitwise_xor(col_index, jnp.asarray(spread, jnp.int32))
    slot_of = jnp.bitwise_xor(col_index, jnp.arange(col_count, dtype=jnp.int32))
    slot_of = jnp.take(jnp.asarray(np.argsort(spread), jnp.int32), slot_of)

    pieces = [diag_blocks] + [
        lax.ppermute(diag_blocks, "prow", [(i, (i + k) % row_count) for i in range(row_count)])
        for k in range(1, row_count)
    ]
    order = (row_index - jnp.arange(row_count, dtype=jnp.int32)) % row_count
    whole_diag = sum(
        jnp.where((order == k)[None, :, None, None], piece[:, None], 0.0)
        for k, piece in enumerate(pieces)
    ).reshape(diag_blocks.shape[0], -1, diag_blocks.shape[2])

    own_map = lax.dynamic_slice_in_dim(child_map, row_index * col_count, col_count, 1)
    table = first_match(own_map - row_index * row_blocks,
                        jnp.arange(row_blocks, dtype=jnp.int32))
    table = jnp.where(table >= 0, jnp.take(slot_of, jnp.maximum(table, 0)), -1)

    first_col = col_index * col_blocks
    source = first_col // row_blocks
    source_map = lax.dynamic_slice_in_dim(child_map, source * col_count, col_count, 1)
    picks = first_match(source_map, first_col + jnp.arange(col_blocks, dtype=jnp.int32))
    keep = (picks >= 0) & (row_index == source)
    select = (picks[:, :, None] == child_at) & keep[:, :, None]
    window = jnp.einsum("pjk,kbpa->pjba", select.astype(jnp.float32),
                        group.reshape(col_count, width, 2, width), precision=HIGHEST)
    window, whole_diag = lax.optimization_barrier((window, whole_diag))
    lower_factor = jnp.linalg.cholesky(whole_diag)
    eye = jnp.broadcast_to(jnp.eye(width, dtype=jnp.float32), whole_diag.shape)
    inverse_factor = lax.linalg.triangular_solve(
        lower_factor, eye, left_side=True, lower=True)
    inverse = jnp.einsum("pca,pcb->pab", inverse_factor, inverse_factor,
                         precision=HIGHEST)
    owner = [(c * col_blocks) // row_blocks for c in range(col_count)]
    window = window + sum(
        lax.ppermute(window, ("prow", "pcol"), [
            (owner[c] * col_count + c, (owner[c] + k) * col_count + c)
            for c in range(col_count) if owner[c] + k < row_count
        ])
        for k in range(1, row_count)
    )
    right = jnp.einsum("pxa,pjba->pxjb", inverse, window, precision=HIGHEST)
    right = right.reshape(2 * width, col_blocks * width)

    place = jnp.stack([row_index, col_index]).astype(jnp.int32)
    return apply_update(table, place, group, right, front, width, row_blocks, col_blocks)


def solution(mesh):
    return jax.shard_map(
        per_device,
        mesh=mesh,
        in_specs=(P(None, "prow", None), P(None, None, ("prow", "pcol")), P(), P("prow", "pcol")),
        out_specs=P("prow", "pcol"),
        check_vma=False,
    )
```

```python
import functools

import jax
import numpy as np
import jax.numpy as jnp
from jax import lax
from jax.experimental import pallas as pl
from jax.experimental.pallas import tpu as pltpu
from jax.sharding import PartitionSpec as P

HIGHEST = lax.Precision.HIGHEST
TILE_ROWS = 512


def split_bf16(value):
    scaled = value * 65537.0
    high = scaled - (scaled - value)
    return high.astype(jnp.bfloat16), (value - high).astype(jnp.bfloat16)


def front_kernel(width, row_blocks, col_blocks, table_ref, place_ref,
                 group_ref, stack_ref, front_ref, out_ref, left_ref):
    step = pl.program_id(0)
    tile_rows, cols = front_ref.shape
    per_tile = tile_rows // width
    first_row = place_ref[0] * row_blocks + step * per_tile
    first_col = place_ref[1] * col_blocks

    def update():
        lane = lax.broadcasted_iota(jnp.int32, (width, 2 * width), 1)
        for local in range(per_tile):
            block = step * per_tile + local
            first = table_ref[0, block]
            second = table_ref[1, block]
            from_first = group_ref[jnp.maximum(first, 0)]
            from_second = group_ref[jnp.maximum(second, 0)]
            left_ref[local * width:(local + 1) * width, :] = jnp.where(
                lane < width,
                jnp.where(first >= 0, from_first, 0.0),
                jnp.where(second >= 0, from_second, 0.0),
            )
        high, low = split_bf16(left_ref[...])
        return jnp.dot(jnp.concatenate([high, high, low], axis=1), stack_ref[...],
                       preferred_element_type=jnp.float32)

    all_upper = first_row + per_tile <= first_col
    all_lower = first_row >= first_col + col_blocks - 1

    @pl.when(all_upper)
    def _():
        out_ref[...] = front_ref[...]

    @pl.when(all_lower)
    def _():
        out_ref[...] = front_ref[...] - update()

    @pl.when(jnp.logical_not(all_upper | all_lower))
    def _():
        rows = first_row * width + lax.broadcasted_iota(jnp.int32, (tile_rows, cols), 0)
        cols_at = first_col * width + lax.broadcasted_iota(jnp.int32, (tile_rows, cols), 1)
        lower = rows >= jnp.bitwise_and(cols_at, -width)
        out_ref[...] = front_ref[...] - jnp.where(lower, update(), 0.0)


def apply_update(table, place, group, right, front, width, row_blocks, col_blocks):
    rows, cols = front.shape
    high, low = split_bf16(right)
    stack = jnp.concatenate([high, low, high], axis=0)
    tiles = rows // TILE_ROWS
    kernel = functools.partial(front_kernel, width, row_blocks, col_blocks)
    return pl.pallas_call(
        kernel,
        out_shape=jax.ShapeDtypeStruct(front.shape, front.dtype),
        grid_spec=pltpu.PrefetchScalarGridSpec(
            num_scalar_prefetch=2,
            grid=(tiles,),
            in_specs=[
                pl.BlockSpec(group.shape, lambda i, t, p: (0, 0, 0)),
                pl.BlockSpec(stack.shape, lambda i, t, p: (0, 0)),
                pl.BlockSpec((TILE_ROWS, cols), lambda i, t, p: (i, 0)),
            ],
            out_specs=pl.BlockSpec((TILE_ROWS, cols), lambda i, t, p: (i, 0)),
            scratch_shapes=[pltpu.VMEM((TILE_ROWS, 2 * width), jnp.float32)],
        ),
        cost_estimate=pl.CostEstimate(
            flops=3 * 2 * rows * cols * 2 * width,
            bytes_accessed=2 * rows * cols * 4 + group.size * 4 + stack.size * 2,
            transcendentals=0,
        ),
    )(table, place, group, stack, front)


def doubling_gather(block, axis, count):
    bits = count.bit_length() - 1
    spread = [0]
    for bit in reversed(range(bits)):
        mask = 1 << bit
        other = lax.ppermute(block, axis, [(i, i ^ mask) for i in range(count)])
        block = jnp.concatenate([block, other], axis=0)
        spread = spread + [s ^ mask for s in spread]
    return block, spread


def first_match(mapping, targets):
    hit = mapping[:, :, None] == targets[None, None, :]
    index = jnp.argmax(hit, axis=1).astype(jnp.int32)
    return jnp.where(jnp.any(hit, axis=1), index, -1)


def per_device(diag_blocks, panel_rows, child_map, front):
    width = panel_rows.shape[1]
    row_index = lax.axis_index("prow")
    col_index = lax.axis_index("pcol")
    col_count = lax.axis_size("pcol")
    row_blocks = front.shape[0] // width
    col_blocks = front.shape[1] // width

    row_count = lax.axis_size("prow")

    local = jnp.transpose(panel_rows, (2, 0, 1)).reshape(width, 2 * width)
    group, spread = doubling_gather(local[None], "pcol", col_count)
    child_at = jnp.bitwise_xor(col_index, jnp.asarray(spread, jnp.int32))
    slot_of = jnp.bitwise_xor(col_index, jnp.arange(col_count, dtype=jnp.int32))
    slot_of = jnp.take(jnp.asarray(np.argsort(spread), jnp.int32), slot_of)

    pieces = [diag_blocks] + [
        lax.ppermute(diag_blocks, "prow", [(i, (i + k) % row_count) for i in range(row_count)])
        for k in range(1, row_count)
    ]
    order = (row_index - jnp.arange(row_count, dtype=jnp.int32)) % row_count
    whole_diag = sum(
        jnp.where((order == k)[None, :, None, None], piece[:, None], 0.0)
        for k, piece in enumerate(pieces)
    ).reshape(diag_blocks.shape[0], -1, diag_blocks.shape[2])

    own_map = lax.dynamic_slice_in_dim(child_map, row_index * col_count, col_count, 1)
    table = first_match(own_map - row_index * row_blocks,
                        jnp.arange(row_blocks, dtype=jnp.int32))
    table = jnp.where(table >= 0, jnp.take(slot_of, jnp.maximum(table, 0)), -1)

    first_col = col_index * col_blocks
    source = first_col // row_blocks
    source_map = lax.dynamic_slice_in_dim(child_map, source * col_count, col_count, 1)
    picks = first_match(source_map, first_col + jnp.arange(col_blocks, dtype=jnp.int32))
    keep = (picks >= 0) & (row_index == source)
    select = (picks[:, :, None] == child_at) & keep[:, :, None]
    window = jnp.einsum("pjk,kbpa->pjba", select.astype(jnp.float32),
                        group.reshape(col_count, width, 2, width), precision=HIGHEST)
    window, whole_diag = lax.optimization_barrier((window, whole_diag))
    lower_factor = jnp.linalg.cholesky(whole_diag)
    eye = jnp.broadcast_to(jnp.eye(width, dtype=jnp.float32), whole_diag.shape)
    inverse_factor = lax.linalg.triangular_solve(
        lower_factor, eye, left_side=True, lower=True)
    inverse = jnp.einsum("pca,pcb->pab", inverse_factor, inverse_factor,
                         precision=HIGHEST)
    owner = [(c * col_blocks) // row_blocks for c in range(col_count)]
    window = window + sum(
        lax.ppermute(window, ("prow", "pcol"), [
            (owner[c] * col_count + c, (owner[c] + k) * col_count + c)
            for c in range(col_count) if owner[c] + k < row_count
        ])
        for k in range(1, row_count)
    )
    right = jnp.einsum("pxa,pjba->pxjb", inverse, window, precision=HIGHEST)
    right = right.reshape(2 * width, col_blocks * width)

    place = jnp.stack([row_index, col_index]).astype(jnp.int32)
    return apply_update(table, place, group, right, front, width, row_blocks, col_blocks)


def solution(mesh):
    return jax.shard_map(
        per_device,
        mesh=mesh,
        in_specs=(P(None, "prow", None), P(None, None, ("prow", "pcol")), P(), P("prow", "pcol")),
        out_specs=P("prow", "pcol"),
        check_vma=False,
    )
```

```python
import functools

import jax
import numpy as np
import jax.numpy as jnp
from jax import lax
from jax.experimental import pallas as pl
from jax.experimental.pallas import tpu as pltpu
from jax.sharding import PartitionSpec as P

HIGHEST = lax.Precision.HIGHEST
TILE_ROWS = 512


def split_bf16(value):
    scaled = value * 65537.0
    high = scaled - (scaled - value)
    return high.astype(jnp.bfloat16), (value - high).astype(jnp.bfloat16)


def front_kernel(width, row_blocks, col_blocks, table_ref, place_ref,
                 near_ref, far_ref, stack_ref, front_ref, out_ref, left_ref):
    step = pl.program_id(0)
    tile_rows, cols = front_ref.shape
    per_tile = tile_rows // width
    half = near_ref.shape[0]

    def held(slot):
        near = near_ref[jnp.clip(slot, 0, half - 1)]
        far = far_ref[jnp.clip(slot - half, 0, half - 1)]
        return jnp.where(slot < half, near, far)

    first_row = place_ref[0] * row_blocks + step * per_tile
    first_col = place_ref[1] * col_blocks

    def update():
        lane = lax.broadcasted_iota(jnp.int32, (width, 2 * width), 1)
        for local in range(per_tile):
            block = step * per_tile + local
            first = table_ref[0, block]
            second = table_ref[1, block]
            from_first = held(first)
            from_second = held(second)
            left_ref[local * width:(local + 1) * width, :] = jnp.where(
                lane < width,
                jnp.where(first >= 0, from_first, 0.0),
                jnp.where(second >= 0, from_second, 0.0),
            )
        high, low = split_bf16(left_ref[...])
        return jnp.dot(jnp.concatenate([high, high, low], axis=1), stack_ref[...],
                       preferred_element_type=jnp.float32)

    all_upper = first_row + per_tile <= first_col
    all_lower = first_row >= first_col + col_blocks - 1

    @pl.when(all_upper)
    def _():
        out_ref[...] = front_ref[...]

    @pl.when(all_lower)
    def _():
        out_ref[...] = front_ref[...] - update()

    @pl.when(jnp.logical_not(all_upper | all_lower))
    def _():
        rows = first_row * width + lax.broadcasted_iota(jnp.int32, (tile_rows, cols), 0)
        cols_at = first_col * width + lax.broadcasted_iota(jnp.int32, (tile_rows, cols), 1)
        lower = rows >= jnp.bitwise_and(cols_at, -width)
        out_ref[...] = front_ref[...] - jnp.where(lower, update(), 0.0)


def apply_update(table, place, near, far, right, front, width, row_blocks, col_blocks):
    rows, cols = front.shape
    high, low = split_bf16(right)
    stack = jnp.concatenate([high, low, high], axis=0)
    tiles = rows // TILE_ROWS
    kernel = functools.partial(front_kernel, width, row_blocks, col_blocks)
    return pl.pallas_call(
        kernel,
        out_shape=jax.ShapeDtypeStruct(front.shape, front.dtype),
        grid_spec=pltpu.PrefetchScalarGridSpec(
            num_scalar_prefetch=2,
            grid=(tiles,),
            in_specs=[
                pl.BlockSpec(near.shape, lambda i, t, p: (0, 0, 0)),
                pl.BlockSpec(far.shape, lambda i, t, p: (0, 0, 0)),
                pl.BlockSpec(stack.shape, lambda i, t, p: (0, 0)),
                pl.BlockSpec((TILE_ROWS, cols), lambda i, t, p: (i, 0)),
            ],
            out_specs=pl.BlockSpec((TILE_ROWS, cols), lambda i, t, p: (i, 0)),
            scratch_shapes=[pltpu.VMEM((TILE_ROWS, 2 * width), jnp.float32)],
        ),
        cost_estimate=pl.CostEstimate(
            flops=3 * 2 * rows * cols * 2 * width,
            bytes_accessed=2 * rows * cols * 4 + 2 * near.size * 4 + stack.size * 2,
            transcendentals=0,
        ),
    )(table, place, near, far, stack, front)


def doubling_gather(block, axis, count):
    bits = count.bit_length() - 1
    spread = [0]
    for bit in reversed(range(bits)):
        mask = 1 << bit
        other = lax.ppermute(block, axis, [(i, i ^ mask) for i in range(count)])
        spread = spread + [s ^ mask for s in spread]
        if bit == 0:
            return block, other, spread
        block = jnp.concatenate([block, other], axis=0)


def first_match(mapping, targets):
    hit = mapping[:, :, None] == targets[None, None, :]
    index = jnp.argmax(hit, axis=1).astype(jnp.int32)
    return jnp.where(jnp.any(hit, axis=1), index, -1)


def per_device(diag_blocks, panel_rows, child_map, front):
    width = panel_rows.shape[1]
    row_index = lax.axis_index("prow")
    col_index = lax.axis_index("pcol")
    col_count = lax.axis_size("pcol")
    row_blocks = front.shape[0] // width
    col_blocks = front.shape[1] // width

    row_count = lax.axis_size("prow")

    local = jnp.transpose(panel_rows, (2, 0, 1)).reshape(width, 2 * width)
    near, far, spread = doubling_gather(local[None], "pcol", col_count)
    half = near.shape[0]
    child_at = jnp.bitwise_xor(col_index, jnp.asarray(spread, jnp.int32))
    slot_of = jnp.bitwise_xor(col_index, jnp.arange(col_count, dtype=jnp.int32))
    slot_of = jnp.take(jnp.asarray(np.argsort(spread), jnp.int32), slot_of)

    pieces = [diag_blocks] + [
        lax.ppermute(diag_blocks, "prow", [(i, (i + k) % row_count) for i in range(row_count)])
        for k in range(1, row_count)
    ]
    order = (row_index - jnp.arange(row_count, dtype=jnp.int32)) % row_count
    whole_diag = sum(
        jnp.where((order == k)[None, :, None, None], piece[:, None], 0.0)
        for k, piece in enumerate(pieces)
    ).reshape(diag_blocks.shape[0], -1, diag_blocks.shape[2])

    own_map = lax.dynamic_slice_in_dim(child_map, row_index * col_count, col_count, 1)
    table = first_match(own_map - row_index * row_blocks,
                        jnp.arange(row_blocks, dtype=jnp.int32))
    table = jnp.where(table >= 0, jnp.take(slot_of, jnp.maximum(table, 0)), -1)

    first_col = col_index * col_blocks
    source = first_col // row_blocks
    source_map = lax.dynamic_slice_in_dim(child_map, source * col_count, col_count, 1)
    picks = first_match(source_map, first_col + jnp.arange(col_blocks, dtype=jnp.int32))
    keep = (picks >= 0) & (row_index == source)
    select = (picks[:, :, None] == child_at) & keep[:, :, None]
    select = select.astype(jnp.float32)
    window = sum(
        jnp.einsum("pjk,kbpa->pjba", select[:, :, part * half:(part + 1) * half],
                   held.reshape(half, width, 2, width), precision=HIGHEST)
        for part, held in enumerate((near, far))
    )
    window, whole_diag = lax.optimization_barrier((window, whole_diag))
    lower_factor = jnp.linalg.cholesky(whole_diag)
    eye = jnp.broadcast_to(jnp.eye(width, dtype=jnp.float32), whole_diag.shape)
    inverse_factor = lax.linalg.triangular_solve(
        lower_factor, eye, left_side=True, lower=True)
    inverse = jnp.einsum("pca,pcb->pab", inverse_factor, inverse_factor,
                         precision=HIGHEST)
    owner = [(c * col_blocks) // row_blocks for c in range(col_count)]
    window = window + sum(
        lax.ppermute(window, ("prow", "pcol"), [
            (owner[c] * col_count + c, (owner[c] + k) * col_count + c)
            for c in range(col_count) if owner[c] + k < row_count
        ])
        for k in range(1, row_count)
    )
    right = jnp.einsum("pxa,pjba->pxjb", inverse, window, precision=HIGHEST)
    right = right.reshape(2 * width, col_blocks * width)

    place = jnp.stack([row_index, col_index]).astype(jnp.int32)
    return apply_update(table, place, near, far, right, front, width, row_blocks, col_blocks)


def solution(mesh):
    return jax.shard_map(
        per_device,
        mesh=mesh,
        in_specs=(P(None, "prow", None), P(None, None, ("prow", "pcol")), P(), P("prow", "pcol")),
        out_specs=P("prow", "pcol"),
        check_vma=False,
    )
```

```python
import functools

import jax
import numpy as np
import jax.numpy as jnp
from jax import lax
from jax.experimental import pallas as pl
from jax.experimental.pallas import tpu as pltpu
from jax.sharding import PartitionSpec as P

HIGHEST = lax.Precision.HIGHEST
TILE_ROWS = 512


def split_bf16(value):
    scaled = value * 65537.0
    high = scaled - (scaled - value)
    return high.astype(jnp.bfloat16), (value - high).astype(jnp.bfloat16)


def front_kernel(width, row_blocks, col_blocks, table_ref, place_ref,
                 near_ref, far_ref, stack_ref, front_ref, out_ref, left_ref):
    step = pl.program_id(0)
    tile_rows, cols = front_ref.shape
    per_tile = tile_rows // width
    half = near_ref.shape[0]

    def held(slot):
        near = near_ref[jnp.clip(slot, 0, half - 1)]
        far = far_ref[jnp.clip(slot - half, 0, half - 1)]
        return jnp.where(slot < half, near, far)

    first_row = place_ref[0] * row_blocks + step * per_tile
    first_col = place_ref[1] * col_blocks

    def update():
        lane = lax.broadcasted_iota(jnp.int32, (width, 2 * width), 1)
        for local in range(per_tile):
            block = step * per_tile + local
            first = table_ref[0, block]
            second = table_ref[1, block]
            from_first = held(first)
            from_second = held(second)
            left_ref[local * width:(local + 1) * width, :] = jnp.where(
                lane < width,
                jnp.where(first >= 0, from_first, 0.0),
                jnp.where(second >= 0, from_second, 0.0),
            )
        high, low = split_bf16(left_ref[...])
        return jnp.dot(jnp.concatenate([high, high, low], axis=1), stack_ref[...],
                       preferred_element_type=jnp.float32)

    all_upper = first_row + per_tile <= first_col
    all_lower = first_row >= first_col + col_blocks - 1

    @pl.when(all_upper)
    def _():
        out_ref[...] = front_ref[...]

    @pl.when(all_lower)
    def _():
        out_ref[...] = front_ref[...] - update()

    @pl.when(jnp.logical_not(all_upper | all_lower))
    def _():
        rows = first_row * width + lax.broadcasted_iota(jnp.int32, (tile_rows, cols), 0)
        cols_at = first_col * width + lax.broadcasted_iota(jnp.int32, (tile_rows, cols), 1)
        lower = rows >= jnp.bitwise_and(cols_at, -width)
        out_ref[...] = front_ref[...] - jnp.where(lower, update(), 0.0)


def apply_update(table, place, near, far, right, front, width, row_blocks, col_blocks):
    rows, cols = front.shape
    high, low = split_bf16(right)
    stack = jnp.concatenate([high, low, high], axis=0)
    tiles = rows // TILE_ROWS
    kernel = functools.partial(front_kernel, width, row_blocks, col_blocks)
    return pl.pallas_call(
        kernel,
        out_shape=jax.ShapeDtypeStruct(front.shape, front.dtype),
        grid_spec=pltpu.PrefetchScalarGridSpec(
            num_scalar_prefetch=2,
            grid=(tiles,),
            in_specs=[
                pl.BlockSpec(near.shape, lambda i, t, p: (0, 0, 0)),
                pl.BlockSpec(far.shape, lambda i, t, p: (0, 0, 0)),
                pl.BlockSpec(stack.shape, lambda i, t, p: (0, 0)),
                pl.BlockSpec((TILE_ROWS, cols), lambda i, t, p: (i, 0)),
            ],
            out_specs=pl.BlockSpec((TILE_ROWS, cols), lambda i, t, p: (i, 0)),
            scratch_shapes=[pltpu.VMEM((TILE_ROWS, 2 * width), jnp.float32)],
        ),
        cost_estimate=pl.CostEstimate(
            flops=3 * 2 * rows * cols * 2 * width,
            bytes_accessed=2 * rows * cols * 4 + 2 * near.size * 4 + stack.size * 2,
            transcendentals=0,
        ),
    )(table, place, near, far, stack, front)


def inverse_kernel(system_ref, out_ref, work_ref):
    order = out_ref.shape[1]
    shape = system_ref.shape
    lane = lax.broadcasted_iota(jnp.int32, shape, 2)
    lane_row = lax.broadcasted_iota(jnp.int32, (shape[0], 1, shape[2]), 2)
    row_at = lax.broadcasted_iota(jnp.int32, shape, 1)
    work_ref[...] = system_ref[...]

    def eliminate(k, carry):
        work = work_ref[...]
        row = work_ref[:, pl.ds(k, 1), :]
        pivot = jnp.sum(jnp.where(lane_row == k, row, 0.0), axis=2, keepdims=True)
        row = row / pivot
        column = jnp.sum(jnp.where(lane == k, work, 0.0), axis=2, keepdims=True)
        work_ref[...] = jnp.where(row_at == k, row, work - column * row)
        return carry

    lax.fori_loop(0, order, eliminate, 0)
    out_ref[...] = work_ref[:, :, order:]


def invert_spd(matrix):
    order = matrix.shape[1]
    symmetric = 0.5 * (matrix + jnp.swapaxes(matrix, 1, 2))
    eye = jnp.broadcast_to(jnp.eye(order, dtype=jnp.float32), matrix.shape)
    system = jnp.concatenate([symmetric, eye], axis=2)
    return pl.pallas_call(
        inverse_kernel,
        out_shape=jax.ShapeDtypeStruct(matrix.shape, jnp.float32),
        in_specs=[pl.BlockSpec(memory_space=pltpu.VMEM)],
        out_specs=pl.BlockSpec(memory_space=pltpu.VMEM),
        scratch_shapes=[pltpu.VMEM(system.shape, jnp.float32)],
        cost_estimate=pl.CostEstimate(
            flops=4 * system.size * order, bytes_accessed=system.size * 6,
            transcendentals=0),
    )(system)


def doubling_gather(block, axis, count):
    bits = count.bit_length() - 1
    spread = [0]
    for bit in reversed(range(bits)):
        mask = 1 << bit
        other = lax.ppermute(block, axis, [(i, i ^ mask) for i in range(count)])
        spread = spread + [s ^ mask for s in spread]
        if bit == 0:
            return block, other, spread
        block = jnp.concatenate([block, other], axis=0)


def first_match(mapping, targets):
    hit = mapping[:, :, None] == targets[None, None, :]
    index = jnp.argmax(hit, axis=1).astype(jnp.int32)
    return jnp.where(jnp.any(hit, axis=1), index, -1)


def per_device(diag_blocks, panel_rows, child_map, front):
    width = panel_rows.shape[1]
    row_index = lax.axis_index("prow")
    col_index = lax.axis_index("pcol")
    col_count = lax.axis_size("pcol")
    row_blocks = front.shape[0] // width
    col_blocks = front.shape[1] // width

    row_count = lax.axis_size("prow")

    local = jnp.transpose(panel_rows, (2, 0, 1)).reshape(width, 2 * width)
    near, far, spread = doubling_gather(local[None], "pcol", col_count)
    half = near.shape[0]
    child_at = jnp.bitwise_xor(col_index, jnp.asarray(spread, jnp.int32))
    slot_of = jnp.bitwise_xor(col_index, jnp.arange(col_count, dtype=jnp.int32))
    slot_of = jnp.take(jnp.asarray(np.argsort(spread), jnp.int32), slot_of)

    pieces = [diag_blocks] + [
        lax.ppermute(diag_blocks, "prow", [(i, (i + k) % row_count) for i in range(row_count)])
        for k in range(1, row_count)
    ]
    order = (row_index - jnp.arange(row_count, dtype=jnp.int32)) % row_count
    whole_diag = sum(
        jnp.where((order == k)[None, :, None, None], piece[:, None], 0.0)
        for k, piece in enumerate(pieces)
    ).reshape(diag_blocks.shape[0], -1, diag_blocks.shape[2])

    own_map = lax.dynamic_slice_in_dim(child_map, row_index * col_count, col_count, 1)
    table = first_match(own_map - row_index * row_blocks,
                        jnp.arange(row_blocks, dtype=jnp.int32))
    table = jnp.where(table >= 0, jnp.take(slot_of, jnp.maximum(table, 0)), -1)

    first_col = col_index * col_blocks
    source = first_col // row_blocks
    source_map = lax.dynamic_slice_in_dim(child_map, source * col_count, col_count, 1)
    picks = first_match(source_map, first_col + jnp.arange(col_blocks, dtype=jnp.int32))
    keep = (picks >= 0) & (row_index == source)
    select = (picks[:, :, None] == child_at) & keep[:, :, None]
    select = select.astype(jnp.float32)
    window = sum(
        jnp.einsum("pjk,kbpa->pjba", select[:, :, part * half:(part + 1) * half],
                   held.reshape(half, width, 2, width), precision=HIGHEST)
        for part, held in enumerate((near, far))
    )
    window, whole_diag = lax.optimization_barrier((window, whole_diag))
    inverse = invert_spd(whole_diag)
    owner = [(c * col_blocks) // row_blocks for c in range(col_count)]
    window = window + sum(
        lax.ppermute(window, ("prow", "pcol"), [
            (owner[c] * col_count + c, (owner[c] + k) * col_count + c)
            for c in range(col_count) if owner[c] + k < row_count
        ])
        for k in range(1, row_count)
    )
    right = jnp.einsum("pxa,pjba->pxjb", inverse, window, precision=HIGHEST)
    right = right.reshape(2 * width, col_blocks * width)

    place = jnp.stack([row_index, col_index]).astype(jnp.int32)
    return apply_update(table, place, near, far, right, front, width, row_blocks, col_blocks)


def solution(mesh):
    return jax.shard_map(
        per_device,
        mesh=mesh,
        in_specs=(P(None, "prow", None), P(None, None, ("prow", "pcol")), P(), P("prow", "pcol")),
        out_specs=P("prow", "pcol"),
        check_vma=False,
    )
```

```python
import functools

import jax
import numpy as np
import jax.numpy as jnp
from jax import lax
from jax.experimental import pallas as pl
from jax.experimental.pallas import tpu as pltpu
from jax.sharding import PartitionSpec as P

HIGHEST = lax.Precision.HIGHEST
TILE_ROWS = 512


def split_bf16(value):
    scaled = value * 65537.0
    high = scaled - (scaled - value)
    return high.astype(jnp.bfloat16), (value - high).astype(jnp.bfloat16)


def front_kernel(width, row_blocks, col_blocks, table_ref, place_ref,
                 near_ref, far_ref, stack_ref, front_ref, out_ref, left_ref):
    step = pl.program_id(0)
    tile_rows, cols = front_ref.shape
    per_tile = tile_rows // width
    half = near_ref.shape[0]

    def held(slot):
        near = near_ref[jnp.clip(slot, 0, half - 1)]
        far = far_ref[jnp.clip(slot - half, 0, half - 1)]
        return jnp.where(slot < half, near, far)

    first_row = place_ref[0] * row_blocks + step * per_tile
    first_col = place_ref[1] * col_blocks

    def update():
        lane = lax.broadcasted_iota(jnp.int32, (width, 2 * width), 1)
        for local in range(per_tile):
            block = step * per_tile + local
            first = table_ref[0, block]
            second = table_ref[1, block]
            from_first = held(first)
            from_second = held(second)
            left_ref[local * width:(local + 1) * width, :] = jnp.where(
                lane < width,
                jnp.where(first >= 0, from_first, 0.0),
                jnp.where(second >= 0, from_second, 0.0),
            )
        high, low = split_bf16(left_ref[...])
        return jnp.dot(jnp.concatenate([high, high, low], axis=1), stack_ref[...],
                       preferred_element_type=jnp.float32)

    all_upper = first_row + per_tile <= first_col
    all_lower = first_row >= first_col + col_blocks - 1

    @pl.when(all_upper)
    def _():
        out_ref[...] = front_ref[...]

    @pl.when(all_lower)
    def _():
        out_ref[...] = front_ref[...] - update()

    @pl.when(jnp.logical_not(all_upper | all_lower))
    def _():
        rows = first_row * width + lax.broadcasted_iota(jnp.int32, (tile_rows, cols), 0)
        cols_at = first_col * width + lax.broadcasted_iota(jnp.int32, (tile_rows, cols), 1)
        lower = rows >= jnp.bitwise_and(cols_at, -width)
        out_ref[...] = front_ref[...] - jnp.where(lower, update(), 0.0)


def apply_update(table, place, near, far, right, front, width, row_blocks, col_blocks):
    rows, cols = front.shape
    high, low = split_bf16(right)
    stack = jnp.concatenate([high, low, high], axis=0)
    tiles = rows // TILE_ROWS
    kernel = functools.partial(front_kernel, width, row_blocks, col_blocks)
    return pl.pallas_call(
        kernel,
        out_shape=jax.ShapeDtypeStruct(front.shape, front.dtype),
        grid_spec=pltpu.PrefetchScalarGridSpec(
            num_scalar_prefetch=2,
            grid=(tiles,),
            in_specs=[
                pl.BlockSpec(near.shape, lambda i, t, p: (0, 0, 0)),
                pl.BlockSpec(far.shape, lambda i, t, p: (0, 0, 0)),
                pl.BlockSpec(stack.shape, lambda i, t, p: (0, 0)),
                pl.BlockSpec((TILE_ROWS, cols), lambda i, t, p: (i, 0)),
            ],
            out_specs=pl.BlockSpec((TILE_ROWS, cols), lambda i, t, p: (i, 0)),
            scratch_shapes=[pltpu.VMEM((TILE_ROWS, 2 * width), jnp.float32)],
        ),
        cost_estimate=pl.CostEstimate(
            flops=3 * 2 * rows * cols * 2 * width,
            bytes_accessed=2 * rows * cols * 4 + 2 * near.size * 4 + stack.size * 2,
            transcendentals=0,
        ),
    )(table, place, near, far, stack, front)


def inverse_kernel(system_ref, out_ref, work_ref):
    order = out_ref.shape[1]
    shape = system_ref.shape
    lane = lax.broadcasted_iota(jnp.int32, shape, 2)
    lane_row = lax.broadcasted_iota(jnp.int32, (shape[0], 1, shape[2]), 2)
    row_at = lax.broadcasted_iota(jnp.int32, shape, 1)
    work_ref[...] = system_ref[...]

    def eliminate(k, carry):
        work = work_ref[...]
        row = work_ref[:, pl.ds(k, 1), :]
        pivot = jnp.sum(jnp.where(lane_row == k, row, 0.0), axis=2, keepdims=True)
        row = row / pivot
        column = jnp.sum(jnp.where(lane == k, work, 0.0), axis=2, keepdims=True)
        work_ref[...] = jnp.where(row_at == k, row, work - column * row)
        return carry

    lax.fori_loop(0, order, eliminate, 0)
    out_ref[...] = work_ref[:, :, order:]


def invert_spd(matrix):
    order = matrix.shape[1]
    symmetric = 0.5 * (matrix + jnp.swapaxes(matrix, 1, 2))
    eye = jnp.broadcast_to(jnp.eye(order, dtype=jnp.float32), matrix.shape)
    system = jnp.concatenate([symmetric, eye], axis=2)
    return pl.pallas_call(
        inverse_kernel,
        out_shape=jax.ShapeDtypeStruct(matrix.shape, jnp.float32),
        in_specs=[pl.BlockSpec(memory_space=pltpu.VMEM)],
        out_specs=pl.BlockSpec(memory_space=pltpu.VMEM),
        scratch_shapes=[pltpu.VMEM(system.shape, jnp.float32)],
        cost_estimate=pl.CostEstimate(
            flops=4 * system.size * order, bytes_accessed=system.size * 6,
            transcendentals=0),
    )(system)


def doubling_gather(block, axis, count):
    bits = count.bit_length() - 1
    spread = [0]
    for bit in reversed(range(bits)):
        mask = 1 << bit
        other = lax.ppermute(block, axis, [(i, i ^ mask) for i in range(count)])
        spread = spread + [s ^ mask for s in spread]
        if bit == 0:
            return block, other, spread
        block = jnp.concatenate([block, other], axis=0)


def first_match(mapping, targets):
    hit = mapping[:, :, None] == targets[None, None, :]
    index = jnp.argmax(hit, axis=1).astype(jnp.int32)
    return jnp.where(jnp.any(hit, axis=1), index, -1)


def per_device(diag_blocks, panel_rows, child_map, front):
    width = panel_rows.shape[1]
    row_index = lax.axis_index("prow")
    col_index = lax.axis_index("pcol")
    col_count = lax.axis_size("pcol")
    row_blocks = front.shape[0] // width
    col_blocks = front.shape[1] // width

    row_count = lax.axis_size("prow")

    local = jnp.transpose(panel_rows, (2, 0, 1)).reshape(width, 2 * width)
    near, far, spread = doubling_gather(local[None], "pcol", col_count)
    half = near.shape[0]
    child_at = jnp.bitwise_xor(col_index, jnp.asarray(spread, jnp.int32))
    slot_of = jnp.bitwise_xor(col_index, jnp.arange(col_count, dtype=jnp.int32))
    slot_of = jnp.take(jnp.asarray(np.argsort(spread), jnp.int32), slot_of)

    pieces = [diag_blocks] + [
        lax.ppermute(diag_blocks, "prow", [(i, (i + k) % row_count) for i in range(row_count)])
        for k in range(1, row_count)
    ]
    order = (row_index - jnp.arange(row_count, dtype=jnp.int32)) % row_count
    whole_diag = sum(
        jnp.where((order == k)[None, :, None, None], piece[:, None], 0.0)
        for k, piece in enumerate(pieces)
    ).reshape(diag_blocks.shape[0], -1, diag_blocks.shape[2])

    first_col = col_index * col_blocks
    source = first_col // row_blocks
    source_map = lax.dynamic_slice_in_dim(child_map, source * col_count, col_count, 1)
    picks = first_match(source_map, first_col + jnp.arange(col_blocks, dtype=jnp.int32))
    keep = (picks >= 0) & (row_index == source)
    select = (picks[:, :, None] == child_at) & keep[:, :, None]
    select = select.astype(jnp.float32)
    window = sum(
        jnp.einsum("pjk,kbpa->pjba", select[:, :, part * half:(part + 1) * half],
                   held.reshape(half, width, 2, width), precision=HIGHEST)
        for part, held in enumerate((near, far))
    )
    window, whole_diag, child_map = lax.optimization_barrier((window, whole_diag, child_map))
    inverse = invert_spd(whole_diag)
    own_map = lax.dynamic_slice_in_dim(child_map, row_index * col_count, col_count, 1)
    table = first_match(own_map - row_index * row_blocks,
                        jnp.arange(row_blocks, dtype=jnp.int32))
    table = jnp.where(table >= 0, jnp.take(slot_of, jnp.maximum(table, 0)), -1)

    owner = [(c * col_blocks) // row_blocks for c in range(col_count)]
    window = window + sum(
        lax.ppermute(window, ("prow", "pcol"), [
            (owner[c] * col_count + c, (owner[c] + k) * col_count + c)
            for c in range(col_count) if owner[c] + k < row_count
        ])
        for k in range(1, row_count)
    )
    right = jnp.einsum("pxa,pjba->pxjb", inverse, window, precision=HIGHEST)
    right = right.reshape(2 * width, col_blocks * width)

    place = jnp.stack([row_index, col_index]).astype(jnp.int32)
    return apply_update(table, place, near, far, right, front, width, row_blocks, col_blocks)


def solution(mesh):
    return jax.shard_map(
        per_device,
        mesh=mesh,
        in_specs=(P(None, "prow", None), P(None, None, ("prow", "pcol")), P(), P("prow", "pcol")),
        out_specs=P("prow", "pcol"),
        check_vma=False,
    )
```

```python
import functools

import jax
import numpy as np
import jax.numpy as jnp
from jax import lax
from jax.experimental import pallas as pl
from jax.experimental.pallas import tpu as pltpu
from jax.sharding import PartitionSpec as P

HIGHEST = lax.Precision.HIGHEST
TILE_ROWS = 512


def split_bf16(value):
    scaled = value * 65537.0
    high = scaled - (scaled - value)
    return high.astype(jnp.bfloat16), (value - high).astype(jnp.bfloat16)


def front_kernel(width, row_blocks, col_blocks, table_ref, place_ref,
                 near_ref, far_ref, stack_ref, front_ref, out_ref, left_ref):
    step = pl.program_id(0)
    tile_rows, cols = front_ref.shape
    per_tile = tile_rows // width
    half = near_ref.shape[0]

    def held(slot):
        near = near_ref[jnp.clip(slot, 0, half - 1)]
        far = far_ref[jnp.clip(slot - half, 0, half - 1)]
        return jnp.where(slot < half, near, far)

    first_row = place_ref[0] * row_blocks + step * per_tile
    first_col = place_ref[1] * col_blocks

    def update():
        lane = lax.broadcasted_iota(jnp.int32, (width, 2 * width), 1)
        for local in range(per_tile):
            block = step * per_tile + local
            first = table_ref[0, block]
            second = table_ref[1, block]
            from_first = held(first)
            from_second = held(second)
            left_ref[local * width:(local + 1) * width, :] = jnp.where(
                lane < width,
                jnp.where(first >= 0, from_first, 0.0),
                jnp.where(second >= 0, from_second, 0.0),
            )
        high, low = split_bf16(left_ref[...])
        return jnp.dot(jnp.concatenate([high, high, low], axis=1), stack_ref[...],
                       preferred_element_type=jnp.float32)

    all_upper = first_row + per_tile <= first_col
    all_lower = first_row >= first_col + col_blocks - 1

    @pl.when(all_upper)
    def _():
        out_ref[...] = front_ref[...]

    @pl.when(all_lower)
    def _():
        out_ref[...] = front_ref[...] - update()

    @pl.when(jnp.logical_not(all_upper | all_lower))
    def _():
        rows = first_row * width + lax.broadcasted_iota(jnp.int32, (tile_rows, cols), 0)
        cols_at = first_col * width + lax.broadcasted_iota(jnp.int32, (tile_rows, cols), 1)
        lower = rows >= jnp.bitwise_and(cols_at, -width)
        out_ref[...] = front_ref[...] - jnp.where(lower, update(), 0.0)


def apply_update(table, place, near, far, right, front, width, row_blocks, col_blocks):
    rows, cols = front.shape
    high, low = split_bf16(right)
    stack = jnp.concatenate([high, low, high], axis=0)
    tiles = rows // TILE_ROWS
    kernel = functools.partial(front_kernel, width, row_blocks, col_blocks)
    return pl.pallas_call(
        kernel,
        out_shape=jax.ShapeDtypeStruct(front.shape, front.dtype),
        grid_spec=pltpu.PrefetchScalarGridSpec(
            num_scalar_prefetch=2,
            grid=(tiles,),
            in_specs=[
                pl.BlockSpec(near.shape, lambda i, t, p: (0, 0, 0)),
                pl.BlockSpec(far.shape, lambda i, t, p: (0, 0, 0)),
                pl.BlockSpec(stack.shape, lambda i, t, p: (0, 0)),
                pl.BlockSpec((TILE_ROWS, cols), lambda i, t, p: (i, 0)),
            ],
            out_specs=pl.BlockSpec((TILE_ROWS, cols), lambda i, t, p: (i, 0)),
            scratch_shapes=[pltpu.VMEM((TILE_ROWS, 2 * width), jnp.float32)],
        ),
        cost_estimate=pl.CostEstimate(
            flops=3 * 2 * rows * cols * 2 * width,
            bytes_accessed=2 * rows * cols * 4 + 2 * near.size * 4 + stack.size * 2,
            transcendentals=0,
        ),
    )(table, place, near, far, stack, front)


def inverse_kernel(system_ref, out_ref, work_ref):
    order = out_ref.shape[1]
    shape = system_ref.shape
    lane = lax.broadcasted_iota(jnp.int32, shape, 2)
    lane_row = lax.broadcasted_iota(jnp.int32, (shape[0], 1, shape[2]), 2)
    row_at = lax.broadcasted_iota(jnp.int32, shape, 1)
    work_ref[...] = system_ref[...]

    def eliminate(k, carry):
        work = work_ref[...]
        row = work_ref[:, pl.ds(k, 1), :]
        pivot = jnp.sum(jnp.where(lane_row == k, row, 0.0), axis=2, keepdims=True)
        row = row / pivot
        column = jnp.sum(jnp.where(lane == k, work, 0.0), axis=2, keepdims=True)
        work_ref[...] = jnp.where(row_at == k, row, work - column * row)
        return carry

    lax.fori_loop(0, order, eliminate, 0)
    out_ref[...] = work_ref[:, :, order:]


def invert_spd(matrix):
    order = matrix.shape[1]
    symmetric = 0.5 * (matrix + jnp.swapaxes(matrix, 1, 2))
    eye = jnp.broadcast_to(jnp.eye(order, dtype=jnp.float32), matrix.shape)
    system = jnp.concatenate([symmetric, eye], axis=2)
    return pl.pallas_call(
        inverse_kernel,
        out_shape=jax.ShapeDtypeStruct(matrix.shape, jnp.float32),
        in_specs=[pl.BlockSpec(memory_space=pltpu.VMEM)],
        out_specs=pl.BlockSpec(memory_space=pltpu.VMEM),
        scratch_shapes=[pltpu.VMEM(system.shape, jnp.float32)],
        cost_estimate=pl.CostEstimate(
            flops=4 * system.size * order, bytes_accessed=system.size * 6,
            transcendentals=0),
    )(system)


def doubling_gather(block, axis, count):
    bits = count.bit_length() - 1
    spread = [0]
    for bit in reversed(range(bits)):
        mask = 1 << bit
        other = lax.ppermute(block, axis, [(i, i ^ mask) for i in range(count)])
        spread = spread + [s ^ mask for s in spread]
        if bit == 0:
            return block, other, spread
        block = jnp.concatenate([block, other], axis=0)


def first_match(mapping, targets):
    hit = mapping[:, :, None] == targets[None, None, :]
    index = jnp.argmax(hit, axis=1).astype(jnp.int32)
    return jnp.where(jnp.any(hit, axis=1), index, -1)


def per_device(diag_blocks, panel_rows, child_map, front):
    width = panel_rows.shape[1]
    row_index = lax.axis_index("prow")
    col_index = lax.axis_index("pcol")
    col_count = lax.axis_size("pcol")
    row_blocks = front.shape[0] // width
    col_blocks = front.shape[1] // width

    row_count = lax.axis_size("prow")

    local = jnp.transpose(panel_rows, (2, 0, 1)).reshape(width, 2 * width)
    near, far, spread = doubling_gather(local[None], "pcol", col_count)
    half = near.shape[0]
    child_at = jnp.bitwise_xor(col_index, jnp.asarray(spread, jnp.int32))
    slot_of = jnp.bitwise_xor(col_index, jnp.arange(col_count, dtype=jnp.int32))
    slot_of = jnp.take(jnp.asarray(np.argsort(spread), jnp.int32), slot_of)

    pieces = [diag_blocks] + [
        lax.ppermute(diag_blocks, "prow", [(i, (i + k) % row_count) for i in range(row_count)])
        for k in range(1, row_count)
    ]
    order = (row_index - jnp.arange(row_count, dtype=jnp.int32)) % row_count
    whole_diag = sum(
        jnp.where((order == k)[None, :, None, None], piece[:, None], 0.0)
        for k, piece in enumerate(pieces)
    ).reshape(diag_blocks.shape[0], -1, diag_blocks.shape[2])

    first_col = col_index * col_blocks
    source = first_col // row_blocks
    source_map = lax.dynamic_slice_in_dim(child_map, source * col_count, col_count, 1)
    picks = first_match(source_map, first_col + jnp.arange(col_blocks, dtype=jnp.int32))
    keep = (picks >= 0) & (row_index == source)
    select = (picks[:, :, None] == child_at) & keep[:, :, None]
    select = select.astype(jnp.float32)
    window = sum(
        jnp.einsum("pjk,kbpa->pjba", select[:, :, part * half:(part + 1) * half],
                   held.reshape(half, width, 2, width), precision=HIGHEST)
        for part, held in enumerate((near, far))
    )
    window, whole_diag, child_map = lax.optimization_barrier((window, whole_diag, child_map))
    inverse = invert_spd(whole_diag)
    own_map = lax.dynamic_slice_in_dim(child_map, row_index * col_count, col_count, 1)
    table = first_match(own_map - row_index * row_blocks,
                        jnp.arange(row_blocks, dtype=jnp.int32))
    table = jnp.where(table >= 0, jnp.take(slot_of, jnp.maximum(table, 0)), -1)

    owner = [(c * col_blocks) // row_blocks for c in range(col_count)]
    def send(value, moves):
        return lax.ppermute(value, ("prow", "pcol"), [
            (a * col_count + c, b * col_count + c) for c, a, b in moves])

    if row_count == 4:
        down = send(window, [(c, owner[c], owner[c] + 1)
                             for c in range(col_count) if owner[c] < 3])
        wrapped = [c for c in range(col_count) if owner[c] < 2]
        back = send(window, [(c, owner[c], (owner[c] - 1) % 4) for c in wrapped])
        relay = send(back, [(c, (owner[c] - 1) % 4, (owner[c] - 2) % 4) for c in wrapped])
        window = window + down + back + relay
    else:
        window = window + sum(
            send(window, [(c, owner[c], owner[c] + k)
                          for c in range(col_count) if owner[c] + k < row_count])
            for k in range(1, row_count)
        )
    right = jnp.einsum("pxa,pjba->pxjb", inverse, window, precision=HIGHEST)
    right = right.reshape(2 * width, col_blocks * width)

    place = jnp.stack([row_index, col_index]).astype(jnp.int32)
    return apply_update(table, place, near, far, right, front, width, row_blocks, col_blocks)


def solution(mesh):
    return jax.shard_map(
        per_device,
        mesh=mesh,
        in_specs=(P(None, "prow", None), P(None, None, ("prow", "pcol")), P(), P("prow", "pcol")),
        out_specs=P("prow", "pcol"),
        check_vma=False,
    )
```

```python
import functools

import jax
import numpy as np
import jax.numpy as jnp
from jax import lax
from jax.experimental import pallas as pl
from jax.experimental.pallas import tpu as pltpu
from jax.sharding import PartitionSpec as P

HIGHEST = lax.Precision.HIGHEST
TILE_ROWS = 512


def split_bf16(value):
    scaled = value * 65537.0
    high = scaled - (scaled - value)
    return high.astype(jnp.bfloat16), (value - high).astype(jnp.bfloat16)


def front_kernel(width, row_blocks, col_blocks, table_ref, place_ref,
                 near_ref, far_ref, stack_ref, front_ref, out_ref, left_ref):
    step = pl.program_id(0)
    tile_rows, cols = front_ref.shape
    per_tile = tile_rows // width
    half = near_ref.shape[0]

    def held(slot):
        near = near_ref[jnp.clip(slot, 0, half - 1)]
        far = far_ref[jnp.clip(slot - half, 0, half - 1)]
        return jnp.where(slot < half, near, far)

    first_row = place_ref[0] * row_blocks + step * per_tile
    first_col = place_ref[1] * col_blocks

    def update():
        lane = lax.broadcasted_iota(jnp.int32, (width, 2 * width), 1)
        for local in range(per_tile):
            block = step * per_tile + local
            first = table_ref[0, block]
            second = table_ref[1, block]
            from_first = held(first)
            from_second = held(second)
            left_ref[local * width:(local + 1) * width, :] = jnp.where(
                lane < width,
                jnp.where(first >= 0, from_first, 0.0),
                jnp.where(second >= 0, from_second, 0.0),
            )
        high, low = split_bf16(left_ref[...])
        return jnp.dot(jnp.concatenate([high, high, low], axis=1), stack_ref[...],
                       preferred_element_type=jnp.float32)

    all_upper = first_row + per_tile <= first_col
    all_lower = first_row >= first_col + col_blocks - 1

    @pl.when(all_upper)
    def _():
        out_ref[...] = front_ref[...]

    @pl.when(all_lower)
    def _():
        out_ref[...] = front_ref[...] - update()

    @pl.when(jnp.logical_not(all_upper | all_lower))
    def _():
        rows = first_row * width + lax.broadcasted_iota(jnp.int32, (tile_rows, cols), 0)
        cols_at = first_col * width + lax.broadcasted_iota(jnp.int32, (tile_rows, cols), 1)
        lower = rows >= jnp.bitwise_and(cols_at, -width)
        out_ref[...] = front_ref[...] - jnp.where(lower, update(), 0.0)


def apply_update(table, place, near, far, right, front, width, row_blocks, col_blocks):
    rows, cols = front.shape
    high, low = split_bf16(right)
    stack = jnp.concatenate([high, low, high], axis=0)
    tiles = rows // TILE_ROWS
    kernel = functools.partial(front_kernel, width, row_blocks, col_blocks)
    return pl.pallas_call(
        kernel,
        out_shape=jax.ShapeDtypeStruct(front.shape, front.dtype),
        grid_spec=pltpu.PrefetchScalarGridSpec(
            num_scalar_prefetch=2,
            grid=(tiles,),
            in_specs=[
                pl.BlockSpec(near.shape, lambda i, t, p: (0, 0, 0)),
                pl.BlockSpec(far.shape, lambda i, t, p: (0, 0, 0)),
                pl.BlockSpec(stack.shape, lambda i, t, p: (0, 0)),
                pl.BlockSpec((TILE_ROWS, cols), lambda i, t, p: (i, 0)),
            ],
            out_specs=pl.BlockSpec((TILE_ROWS, cols), lambda i, t, p: (i, 0)),
            scratch_shapes=[pltpu.VMEM((TILE_ROWS, 2 * width), jnp.float32)],
        ),
        cost_estimate=pl.CostEstimate(
            flops=3 * 2 * rows * cols * 2 * width,
            bytes_accessed=2 * rows * cols * 4 + 2 * near.size * 4 + stack.size * 2,
            transcendentals=0,
        ),
    )(table, place, near, far, stack, front)


def inverse_kernel(system_ref, out_ref, work_ref):
    order = out_ref.shape[1]
    shape = system_ref.shape
    lane = lax.broadcasted_iota(jnp.int32, shape, 2)
    lane_row = lax.broadcasted_iota(jnp.int32, (shape[0], 1, shape[2]), 2)
    row_at = lax.broadcasted_iota(jnp.int32, shape, 1)
    work_ref[...] = system_ref[...]

    def eliminate(k, carry):
        work = work_ref[...]
        row = work_ref[:, pl.ds(k, 1), :]
        pivot = jnp.sum(jnp.where(lane_row == k, row, 0.0), axis=2, keepdims=True)
        row = row / pivot
        column = jnp.sum(jnp.where(lane == k, work, 0.0), axis=2, keepdims=True)
        work_ref[...] = jnp.where(row_at == k, row, work - column * row)
        return carry

    lax.fori_loop(0, order, eliminate, 0)
    out_ref[...] = work_ref[:, :, order:]


def invert_spd(matrix):
    order = matrix.shape[1]
    symmetric = 0.5 * (matrix + jnp.swapaxes(matrix, 1, 2))
    eye = jnp.broadcast_to(jnp.eye(order, dtype=jnp.float32), matrix.shape)
    system = jnp.concatenate([symmetric, eye], axis=2)
    return pl.pallas_call(
        inverse_kernel,
        out_shape=jax.ShapeDtypeStruct(matrix.shape, jnp.float32),
        in_specs=[pl.BlockSpec(memory_space=pltpu.VMEM)],
        out_specs=pl.BlockSpec(memory_space=pltpu.VMEM),
        scratch_shapes=[pltpu.VMEM(system.shape, jnp.float32)],
        cost_estimate=pl.CostEstimate(
            flops=4 * system.size * order, bytes_accessed=system.size * 6,
            transcendentals=0),
    )(system)


def doubling_gather(block, axis, count):
    bits = count.bit_length() - 1
    spread = [0]
    for bit in reversed(range(bits)):
        mask = 1 << bit
        other = lax.ppermute(block, axis, [(i, i ^ mask) for i in range(count)])
        spread = spread + [s ^ mask for s in spread]
        if bit == 0:
            return block, other, spread
        block = jnp.concatenate([block, other], axis=0)


def first_match(mapping, targets):
    hit = mapping[:, :, None] == targets[None, None, :]
    index = jnp.argmax(hit, axis=1).astype(jnp.int32)
    return jnp.where(jnp.any(hit, axis=1), index, -1)


def per_device(diag_blocks, panel_rows, child_map, front):
    width = panel_rows.shape[1]
    row_index = lax.axis_index("prow")
    col_index = lax.axis_index("pcol")
    col_count = lax.axis_size("pcol")
    row_blocks = front.shape[0] // width
    col_blocks = front.shape[1] // width

    row_count = lax.axis_size("prow")

    local = jnp.transpose(panel_rows, (2, 0, 1)).reshape(width, 2 * width)
    near, far, spread = doubling_gather(local[None], "pcol", col_count)
    half = near.shape[0]
    child_at = jnp.bitwise_xor(col_index, jnp.asarray(spread, jnp.int32))
    slot_of = jnp.bitwise_xor(col_index, jnp.arange(col_count, dtype=jnp.int32))
    slot_of = jnp.take(jnp.asarray(np.argsort(spread), jnp.int32), slot_of)

    pieces = [diag_blocks] + [
        lax.ppermute(diag_blocks, "prow", [(i, (i + k) % row_count) for i in range(row_count)])
        for k in range(1, row_count)
    ]
    order = (row_index - jnp.arange(row_count, dtype=jnp.int32)) % row_count
    whole_diag = sum(
        jnp.where((order == k)[None, :, None, None], piece[:, None], 0.0)
        for k, piece in enumerate(pieces)
    ).reshape(diag_blocks.shape[0], -1, diag_blocks.shape[2])

    first_col = col_index * col_blocks
    source = first_col // row_blocks
    source_map = lax.dynamic_slice_in_dim(child_map, source * col_count, col_count, 1)
    picks = first_match(source_map, first_col + jnp.arange(col_blocks, dtype=jnp.int32))
    keep = (picks >= 0) & (row_index == source)
    select = (picks[:, :, None] == child_at) & keep[:, :, None]
    select = select.astype(jnp.float32)
    window = sum(
        jnp.einsum("pjk,kbpa->pjba", select[:, :, part * half:(part + 1) * half],
                   held.reshape(half, width, 2, width), precision=HIGHEST)
        for part, held in enumerate((near, far))
    )
    window, whole_diag, child_map = lax.optimization_barrier((window, whole_diag, child_map))
    inverse = invert_spd(whole_diag)
    own_map = lax.dynamic_slice_in_dim(child_map, row_index * col_count, col_count, 1)
    table = first_match(own_map - row_index * row_blocks,
                        jnp.arange(row_blocks, dtype=jnp.int32))
    table = jnp.where(table >= 0, jnp.take(slot_of, jnp.maximum(table, 0)), -1)

    owner = [(c * col_blocks) // row_blocks for c in range(col_count)]
    def send(value, k):
        return lax.ppermute(value, ("prow", "pcol"), [
            (owner[c] * col_count + c, (owner[c] + k) * col_count + c)
            for c in range(col_count) if owner[c] + k < row_count
        ])

    nearest = jnp.stack([send(window[panel], 1) for panel in range(window.shape[0])])
    window = window + nearest + sum(send(window, k) for k in range(2, row_count))
    right = jnp.einsum("pxa,pjba->pxjb", inverse, window, precision=HIGHEST)
    right = right.reshape(2 * width, col_blocks * width)

    place = jnp.stack([row_index, col_index]).astype(jnp.int32)
    return apply_update(table, place, near, far, right, front, width, row_blocks, col_blocks)


def solution(mesh):
    return jax.shard_map(
        per_device,
        mesh=mesh,
        in_specs=(P(None, "prow", None), P(None, None, ("prow", "pcol")), P(), P("prow", "pcol")),
        out_specs=P("prow", "pcol"),
        check_vma=False,
    )
```

```python
import functools

import jax
import numpy as np
import jax.numpy as jnp
from jax import lax
from jax.experimental import pallas as pl
from jax.experimental.pallas import tpu as pltpu
from jax.sharding import PartitionSpec as P

HIGHEST = lax.Precision.HIGHEST
TILE_ROWS = 512


def split_bf16(value):
    scaled = value * 65537.0
    high = scaled - (scaled - value)
    return high.astype(jnp.bfloat16), (value - high).astype(jnp.bfloat16)


def front_kernel(width, row_blocks, col_blocks, table_ref, place_ref,
                 near_ref, far_ref, stack_ref, front_ref, out_ref, left_ref):
    step = pl.program_id(0)
    tile_rows, cols = front_ref.shape
    per_tile = tile_rows // width
    half = near_ref.shape[0]

    def held(slot):
        near = near_ref[jnp.clip(slot, 0, half - 1)]
        far = far_ref[jnp.clip(slot - half, 0, half - 1)]
        return jnp.where(slot < half, near, far)

    first_row = place_ref[0] * row_blocks + step * per_tile
    first_col = place_ref[1] * col_blocks

    def update():
        lane = lax.broadcasted_iota(jnp.int32, (width, 2 * width), 1)
        for local in range(per_tile):
            block = step * per_tile + local
            first = table_ref[0, block]
            second = table_ref[1, block]
            from_first = held(first)
            from_second = held(second)
            left_ref[local * width:(local + 1) * width, :] = jnp.where(
                lane < width,
                jnp.where(first >= 0, from_first, 0.0),
                jnp.where(second >= 0, from_second, 0.0),
            )
        high, low = split_bf16(left_ref[...])
        return jnp.dot(jnp.concatenate([high, high, low], axis=1), stack_ref[...],
                       preferred_element_type=jnp.float32)

    all_upper = first_row + per_tile <= first_col
    all_lower = first_row >= first_col + col_blocks - 1

    @pl.when(all_upper)
    def _():
        out_ref[...] = front_ref[...]

    @pl.when(all_lower)
    def _():
        out_ref[...] = front_ref[...] - update()

    @pl.when(jnp.logical_not(all_upper | all_lower))
    def _():
        rows = first_row * width + lax.broadcasted_iota(jnp.int32, (tile_rows, cols), 0)
        cols_at = first_col * width + lax.broadcasted_iota(jnp.int32, (tile_rows, cols), 1)
        lower = rows >= jnp.bitwise_and(cols_at, -width)
        out_ref[...] = front_ref[...] - jnp.where(lower, update(), 0.0)


def apply_update(table, place, near, far, right, front, width, row_blocks, col_blocks):
    rows, cols = front.shape
    high, low = split_bf16(right)
    stack = jnp.concatenate([high, low, high], axis=0)
    tiles = rows // TILE_ROWS
    kernel = functools.partial(front_kernel, width, row_blocks, col_blocks)
    return pl.pallas_call(
        kernel,
        out_shape=jax.ShapeDtypeStruct(front.shape, front.dtype),
        grid_spec=pltpu.PrefetchScalarGridSpec(
            num_scalar_prefetch=2,
            grid=(tiles,),
            in_specs=[
                pl.BlockSpec(near.shape, lambda i, t, p: (0, 0, 0)),
                pl.BlockSpec(far.shape, lambda i, t, p: (0, 0, 0)),
                pl.BlockSpec(stack.shape, lambda i, t, p: (0, 0)),
                pl.BlockSpec((TILE_ROWS, cols), lambda i, t, p: (i, 0)),
            ],
            out_specs=pl.BlockSpec((TILE_ROWS, cols), lambda i, t, p: (i, 0)),
            scratch_shapes=[pltpu.VMEM((TILE_ROWS, 2 * width), jnp.float32)],
        ),
        cost_estimate=pl.CostEstimate(
            flops=3 * 2 * rows * cols * 2 * width,
            bytes_accessed=2 * rows * cols * 4 + 2 * near.size * 4 + stack.size * 2,
            transcendentals=0,
        ),
    )(table, place, near, far, stack, front)


def inverse_kernel(system_ref, out_ref, work_ref):
    order = out_ref.shape[1]
    shape = system_ref.shape
    lane = lax.broadcasted_iota(jnp.int32, shape, 2)
    lane_row = lax.broadcasted_iota(jnp.int32, (shape[0], 1, shape[2]), 2)
    row_at = lax.broadcasted_iota(jnp.int32, shape, 1)
    work_ref[...] = system_ref[...]

    def eliminate(k, carry):
        work = work_ref[...]
        row = work_ref[:, pl.ds(k, 1), :]
        pivot = jnp.sum(jnp.where(lane_row == k, row, 0.0), axis=2, keepdims=True)
        row = row / pivot
        column = jnp.sum(jnp.where(lane == k, work, 0.0), axis=2, keepdims=True)
        work_ref[...] = jnp.where(row_at == k, row, work - column * row)
        return carry

    lax.fori_loop(0, order, eliminate, 0)
    out_ref[...] = work_ref[:, :, order:]


def invert_spd(matrix):
    order = matrix.shape[1]
    symmetric = 0.5 * (matrix + jnp.swapaxes(matrix, 1, 2))
    eye = jnp.broadcast_to(jnp.eye(order, dtype=jnp.float32), matrix.shape)
    system = jnp.concatenate([symmetric, eye], axis=2)
    return pl.pallas_call(
        inverse_kernel,
        out_shape=jax.ShapeDtypeStruct(matrix.shape, jnp.float32),
        in_specs=[pl.BlockSpec(memory_space=pltpu.VMEM)],
        out_specs=pl.BlockSpec(memory_space=pltpu.VMEM),
        scratch_shapes=[pltpu.VMEM(system.shape, jnp.float32)],
        cost_estimate=pl.CostEstimate(
            flops=4 * system.size * order, bytes_accessed=system.size * 6,
            transcendentals=0),
    )(system)


def doubling_gather(block, axis, count):
    bits = count.bit_length() - 1
    spread = [0]
    first = None
    for bit in reversed(range(bits)):
        mask = 1 << bit
        other = lax.ppermute(block, axis, [(i, i ^ mask) for i in range(count)])
        first = other if first is None else first
        spread = spread + [s ^ mask for s in spread]
        if bit == 0:
            return block, other, spread, first
        block = jnp.concatenate([block, other], axis=0)


def first_match(mapping, targets):
    hit = mapping[:, :, None] == targets[None, None, :]
    index = jnp.argmax(hit, axis=1).astype(jnp.int32)
    return jnp.where(jnp.any(hit, axis=1), index, -1)


def per_device(diag_blocks, panel_rows, child_map, front):
    width = panel_rows.shape[1]
    row_index = lax.axis_index("prow")
    col_index = lax.axis_index("pcol")
    col_count = lax.axis_size("pcol")
    row_blocks = front.shape[0] // width
    col_blocks = front.shape[1] // width

    row_count = lax.axis_size("prow")

    local = jnp.transpose(panel_rows, (2, 0, 1)).reshape(width, 2 * width)
    near, far, spread, first = doubling_gather(local[None], "pcol", col_count)
    first, diag_blocks = lax.optimization_barrier((first, diag_blocks))
    half = near.shape[0]
    child_at = jnp.bitwise_xor(col_index, jnp.asarray(spread, jnp.int32))
    slot_of = jnp.bitwise_xor(col_index, jnp.arange(col_count, dtype=jnp.int32))
    slot_of = jnp.take(jnp.asarray(np.argsort(spread), jnp.int32), slot_of)

    pieces = [diag_blocks] + [
        lax.ppermute(diag_blocks, "prow", [(i, (i + k) % row_count) for i in range(row_count)])
        for k in range(1, row_count)
    ]
    order = (row_index - jnp.arange(row_count, dtype=jnp.int32)) % row_count
    whole_diag = sum(
        jnp.where((order == k)[None, :, None, None], piece[:, None], 0.0)
        for k, piece in enumerate(pieces)
    ).reshape(diag_blocks.shape[0], -1, diag_blocks.shape[2])

    first_col = col_index * col_blocks
    source = first_col // row_blocks
    source_map = lax.dynamic_slice_in_dim(child_map, source * col_count, col_count, 1)
    picks = first_match(source_map, first_col + jnp.arange(col_blocks, dtype=jnp.int32))
    keep = (picks >= 0) & (row_index == source)
    select = (picks[:, :, None] == child_at) & keep[:, :, None]
    select = select.astype(jnp.float32)
    window = sum(
        jnp.einsum("pjk,kbpa->pjba", select[:, :, part * half:(part + 1) * half],
                   held.reshape(half, width, 2, width), precision=HIGHEST)
        for part, held in enumerate((near, far))
    )
    window, whole_diag, child_map = lax.optimization_barrier((window, whole_diag, child_map))
    inverse = invert_spd(whole_diag)
    own_map = lax.dynamic_slice_in_dim(child_map, row_index * col_count, col_count, 1)
    table = first_match(own_map - row_index * row_blocks,
                        jnp.arange(row_blocks, dtype=jnp.int32))
    table = jnp.where(table >= 0, jnp.take(slot_of, jnp.maximum(table, 0)), -1)

    owner = [(c * col_blocks) // row_blocks for c in range(col_count)]
    def send(value, k):
        return lax.ppermute(value, ("prow", "pcol"), [
            (owner[c] * col_count + c, (owner[c] + k) * col_count + c)
            for c in range(col_count) if owner[c] + k < row_count
        ])

    nearest = jnp.stack([send(window[panel], 1) for panel in range(window.shape[0])])
    window = window + nearest + sum(send(window, k) for k in range(2, row_count))
    right = jnp.einsum("pxa,pjba->pxjb", inverse, window, precision=HIGHEST)
    right = right.reshape(2 * width, col_blocks * width)

    place = jnp.stack([row_index, col_index]).astype(jnp.int32)
    return apply_update(table, place, near, far, right, front, width, row_blocks, col_blocks)


def solution(mesh):
    return jax.shard_map(
        per_device,
        mesh=mesh,
        in_specs=(P(None, "prow", None), P(None, None, ("prow", "pcol")), P(), P("prow", "pcol")),
        out_specs=P("prow", "pcol"),
        check_vma=False,
    )
```

```python
import functools

import jax
import numpy as np
import jax.numpy as jnp
from jax import lax
from jax.experimental import pallas as pl
from jax.experimental.pallas import tpu as pltpu
from jax.sharding import PartitionSpec as P

HIGHEST = lax.Precision.HIGHEST
TILE_ROWS = 256


def split_bf16(value):
    scaled = value * 65537.0
    high = scaled - (scaled - value)
    return high.astype(jnp.bfloat16), (value - high).astype(jnp.bfloat16)


def front_kernel(width, row_blocks, col_blocks, table_ref, place_ref,
                 near_ref, far_ref, stack_ref, front_ref, out_ref, left_ref):
    step = pl.program_id(0)
    tile_rows, cols = front_ref.shape
    per_tile = tile_rows // width
    half = near_ref.shape[0]

    def held(slot):
        near = near_ref[jnp.clip(slot, 0, half - 1)]
        far = far_ref[jnp.clip(slot - half, 0, half - 1)]
        return jnp.where(slot < half, near, far)

    first_row = place_ref[0] * row_blocks + step * per_tile
    first_col = place_ref[1] * col_blocks

    def update():
        lane = lax.broadcasted_iota(jnp.int32, (width, 2 * width), 1)
        for local in range(per_tile):
            block = step * per_tile + local
            first = table_ref[0, block]
            second = table_ref[1, block]
            from_first = held(first)
            from_second = held(second)
            left_ref[local * width:(local + 1) * width, :] = jnp.where(
                lane < width,
                jnp.where(first >= 0, from_first, 0.0),
                jnp.where(second >= 0, from_second, 0.0),
            )
        high, low = split_bf16(left_ref[...])
        return jnp.dot(jnp.concatenate([high, high, low], axis=1), stack_ref[...],
                       preferred_element_type=jnp.float32)

    all_upper = first_row + per_tile <= first_col
    all_lower = first_row >= first_col + col_blocks - 1

    @pl.when(all_upper)
    def _():
        out_ref[...] = front_ref[...]

    @pl.when(all_lower)
    def _():
        out_ref[...] = front_ref[...] - update()

    @pl.when(jnp.logical_not(all_upper | all_lower))
    def _():
        rows = first_row * width + lax.broadcasted_iota(jnp.int32, (tile_rows, cols), 0)
        cols_at = first_col * width + lax.broadcasted_iota(jnp.int32, (tile_rows, cols), 1)
        lower = rows >= jnp.bitwise_and(cols_at, -width)
        out_ref[...] = front_ref[...] - jnp.where(lower, update(), 0.0)


def apply_update(table, place, near, far, right, front, width, row_blocks, col_blocks):
    rows, cols = front.shape
    high, low = split_bf16(right)
    stack = jnp.concatenate([high, low, high], axis=0)
    tiles = rows // TILE_ROWS
    kernel = functools.partial(front_kernel, width, row_blocks, col_blocks)
    return pl.pallas_call(
        kernel,
        out_shape=jax.ShapeDtypeStruct(front.shape, front.dtype),
        grid_spec=pltpu.PrefetchScalarGridSpec(
            num_scalar_prefetch=2,
            grid=(tiles,),
            in_specs=[
                pl.BlockSpec(near.shape, lambda i, t, p: (0, 0, 0)),
                pl.BlockSpec(far.shape, lambda i, t, p: (0, 0, 0)),
                pl.BlockSpec(stack.shape, lambda i, t, p: (0, 0)),
                pl.BlockSpec((TILE_ROWS, cols), lambda i, t, p: (i, 0)),
            ],
            out_specs=pl.BlockSpec((TILE_ROWS, cols), lambda i, t, p: (i, 0)),
            scratch_shapes=[pltpu.VMEM((TILE_ROWS, 2 * width), jnp.float32)],
        ),
        cost_estimate=pl.CostEstimate(
            flops=3 * 2 * rows * cols * 2 * width,
            bytes_accessed=2 * rows * cols * 4 + 2 * near.size * 4 + stack.size * 2,
            transcendentals=0,
        ),
    )(table, place, near, far, stack, front)


def inverse_kernel(system_ref, out_ref, work_ref):
    order = out_ref.shape[1]
    shape = system_ref.shape
    lane = lax.broadcasted_iota(jnp.int32, shape, 2)
    lane_row = lax.broadcasted_iota(jnp.int32, (shape[0], 1, shape[2]), 2)
    row_at = lax.broadcasted_iota(jnp.int32, shape, 1)
    work_ref[...] = system_ref[...]

    def eliminate(k, carry):
        work = work_ref[...]
        row = work_ref[:, pl.ds(k, 1), :]
        pivot = jnp.sum(jnp.where(lane_row == k, row, 0.0), axis=2, keepdims=True)
        row = row / pivot
        column = jnp.sum(jnp.where(lane == k, work, 0.0), axis=2, keepdims=True)
        work_ref[...] = jnp.where(row_at == k, row, work - column * row)
        return carry

    lax.fori_loop(0, order, eliminate, 0)
    out_ref[...] = work_ref[:, :, order:]


def invert_spd(matrix):
    order = matrix.shape[1]
    symmetric = 0.5 * (matrix + jnp.swapaxes(matrix, 1, 2))
    eye = jnp.broadcast_to(jnp.eye(order, dtype=jnp.float32), matrix.shape)
    system = jnp.concatenate([symmetric, eye], axis=2)
    return pl.pallas_call(
        inverse_kernel,
        out_shape=jax.ShapeDtypeStruct(matrix.shape, jnp.float32),
        in_specs=[pl.BlockSpec(memory_space=pltpu.VMEM)],
        out_specs=pl.BlockSpec(memory_space=pltpu.VMEM),
        scratch_shapes=[pltpu.VMEM(system.shape, jnp.float32)],
        cost_estimate=pl.CostEstimate(
            flops=4 * system.size * order, bytes_accessed=system.size * 6,
            transcendentals=0),
    )(system)


def doubling_gather(block, axis, count):
    bits = count.bit_length() - 1
    spread = [0]
    first = None
    for bit in reversed(range(bits)):
        mask = 1 << bit
        other = lax.ppermute(block, axis, [(i, i ^ mask) for i in range(count)])
        first = other if first is None else first
        spread = spread + [s ^ mask for s in spread]
        if bit == 0:
            return block, other, spread, first
        block = jnp.concatenate([block, other], axis=0)


def first_match(mapping, targets):
    hit = mapping[:, :, None] == targets[None, None, :]
    index = jnp.argmax(hit, axis=1).astype(jnp.int32)
    return jnp.where(jnp.any(hit, axis=1), index, -1)


def per_device(diag_blocks, panel_rows, child_map, front):
    width = panel_rows.shape[1]
    row_index = lax.axis_index("prow")
    col_index = lax.axis_index("pcol")
    col_count = lax.axis_size("pcol")
    row_blocks = front.shape[0] // width
    col_blocks = front.shape[1] // width

    row_count = lax.axis_size("prow")

    local = jnp.transpose(panel_rows, (2, 0, 1)).reshape(width, 2 * width)
    near, far, spread, first = doubling_gather(local[None], "pcol", col_count)
    first, diag_blocks = lax.optimization_barrier((first, diag_blocks))
    half = near.shape[0]
    child_at = jnp.bitwise_xor(col_index, jnp.asarray(spread, jnp.int32))
    slot_of = jnp.bitwise_xor(col_index, jnp.arange(col_count, dtype=jnp.int32))
    slot_of = jnp.take(jnp.asarray(np.argsort(spread), jnp.int32), slot_of)

    pieces = [diag_blocks] + [
        lax.ppermute(diag_blocks, "prow", [(i, (i + k) % row_count) for i in range(row_count)])
        for k in range(1, row_count)
    ]
    order = (row_index - jnp.arange(row_count, dtype=jnp.int32)) % row_count
    whole_diag = sum(
        jnp.where((order == k)[None, :, None, None], piece[:, None], 0.0)
        for k, piece in enumerate(pieces)
    ).reshape(diag_blocks.shape[0], -1, diag_blocks.shape[2])

    first_col = col_index * col_blocks
    source = first_col // row_blocks
    source_map = lax.dynamic_slice_in_dim(child_map, source * col_count, col_count, 1)
    picks = first_match(source_map, first_col + jnp.arange(col_blocks, dtype=jnp.int32))
    keep = (picks >= 0) & (row_index == source)
    select = (picks[:, :, None] == child_at) & keep[:, :, None]
    select = select.astype(jnp.float32)
    window = sum(
        jnp.einsum("pjk,kbpa->pjba", select[:, :, part * half:(part + 1) * half],
                   held.reshape(half, width, 2, width), precision=HIGHEST)
        for part, held in enumerate((near, far))
    )
    window, whole_diag, child_map = lax.optimization_barrier((window, whole_diag, child_map))
    inverse = invert_spd(whole_diag)
    own_map = lax.dynamic_slice_in_dim(child_map, row_index * col_count, col_count, 1)
    table = first_match(own_map - row_index * row_blocks,
                        jnp.arange(row_blocks, dtype=jnp.int32))
    table = jnp.where(table >= 0, jnp.take(slot_of, jnp.maximum(table, 0)), -1)

    owner = [(c * col_blocks) // row_blocks for c in range(col_count)]
    def send(value, k):
        return lax.ppermute(value, ("prow", "pcol"), [
            (owner[c] * col_count + c, (owner[c] + k) * col_count + c)
            for c in range(col_count) if owner[c] + k < row_count
        ])

    nearest = jnp.stack([send(window[panel], 1) for panel in range(window.shape[0])])
    window = window + nearest + sum(send(window, k) for k in range(2, row_count))
    right = jnp.einsum("pxa,pjba->pxjb", inverse, window, precision=HIGHEST)
    right = right.reshape(2 * width, col_blocks * width)

    place = jnp.stack([row_index, col_index]).astype(jnp.int32)
    return apply_update(table, place, near, far, right, front, width, row_blocks, col_blocks)


def solution(mesh):
    return jax.shard_map(
        per_device,
        mesh=mesh,
        in_specs=(P(None, "prow", None), P(None, None, ("prow", "pcol")), P(), P("prow", "pcol")),
        out_specs=P("prow", "pcol"),
        check_vma=False,
    )
```

```python
import functools

import jax
import numpy as np
import jax.numpy as jnp
from jax import lax
from jax.experimental import pallas as pl
from jax.experimental.pallas import tpu as pltpu
from jax.sharding import PartitionSpec as P

HIGHEST = lax.Precision.HIGHEST
TILE_ROWS = 1024


def split_bf16(value):
    scaled = value * 65537.0
    high = scaled - (scaled - value)
    return high.astype(jnp.bfloat16), (value - high).astype(jnp.bfloat16)


def front_kernel(width, row_blocks, col_blocks, table_ref, place_ref,
                 near_ref, far_ref, stack_ref, front_ref, out_ref, left_ref):
    step = pl.program_id(0)
    tile_rows, cols = front_ref.shape
    per_tile = tile_rows // width
    half = near_ref.shape[0]

    def held(slot):
        near = near_ref[jnp.clip(slot, 0, half - 1)]
        far = far_ref[jnp.clip(slot - half, 0, half - 1)]
        return jnp.where(slot < half, near, far)

    first_row = place_ref[0] * row_blocks + step * per_tile
    first_col = place_ref[1] * col_blocks

    def update():
        lane = lax.broadcasted_iota(jnp.int32, (width, 2 * width), 1)
        for local in range(per_tile):
            block = step * per_tile + local
            first = table_ref[0, block]
            second = table_ref[1, block]
            from_first = held(first)
            from_second = held(second)
            left_ref[local * width:(local + 1) * width, :] = jnp.where(
                lane < width,
                jnp.where(first >= 0, from_first, 0.0),
                jnp.where(second >= 0, from_second, 0.0),
            )
        high, low = split_bf16(left_ref[...])
        return jnp.dot(jnp.concatenate([high, high, low], axis=1), stack_ref[...],
                       preferred_element_type=jnp.float32)

    all_upper = first_row + per_tile <= first_col
    all_lower = first_row >= first_col + col_blocks - 1

    @pl.when(all_upper)
    def _():
        out_ref[...] = front_ref[...]

    @pl.when(all_lower)
    def _():
        out_ref[...] = front_ref[...] - update()

    @pl.when(jnp.logical_not(all_upper | all_lower))
    def _():
        rows = first_row * width + lax.broadcasted_iota(jnp.int32, (tile_rows, cols), 0)
        cols_at = first_col * width + lax.broadcasted_iota(jnp.int32, (tile_rows, cols), 1)
        lower = rows >= jnp.bitwise_and(cols_at, -width)
        out_ref[...] = front_ref[...] - jnp.where(lower, update(), 0.0)


def apply_update(table, place, near, far, right, front, width, row_blocks, col_blocks):
    rows, cols = front.shape
    high, low = split_bf16(right)
    stack = jnp.concatenate([high, low, high], axis=0)
    tiles = rows // TILE_ROWS
    kernel = functools.partial(front_kernel, width, row_blocks, col_blocks)
    return pl.pallas_call(
        kernel,
        out_shape=jax.ShapeDtypeStruct(front.shape, front.dtype),
        grid_spec=pltpu.PrefetchScalarGridSpec(
            num_scalar_prefetch=2,
            grid=(tiles,),
            in_specs=[
                pl.BlockSpec(near.shape, lambda i, t, p: (0, 0, 0)),
                pl.BlockSpec(far.shape, lambda i, t, p: (0, 0, 0)),
                pl.BlockSpec(stack.shape, lambda i, t, p: (0, 0)),
                pl.BlockSpec((TILE_ROWS, cols), lambda i, t, p: (i, 0)),
            ],
            out_specs=pl.BlockSpec((TILE_ROWS, cols), lambda i, t, p: (i, 0)),
            scratch_shapes=[pltpu.VMEM((TILE_ROWS, 2 * width), jnp.float32)],
        ),
        cost_estimate=pl.CostEstimate(
            flops=3 * 2 * rows * cols * 2 * width,
            bytes_accessed=2 * rows * cols * 4 + 2 * near.size * 4 + stack.size * 2,
            transcendentals=0,
        ),
    )(table, place, near, far, stack, front)


def inverse_kernel(system_ref, out_ref, work_ref):
    order = out_ref.shape[1]
    shape = system_ref.shape
    lane = lax.broadcasted_iota(jnp.int32, shape, 2)
    lane_row = lax.broadcasted_iota(jnp.int32, (shape[0], 1, shape[2]), 2)
    row_at = lax.broadcasted_iota(jnp.int32, shape, 1)
    work_ref[...] = system_ref[...]

    def eliminate(k, carry):
        work = work_ref[...]
        row = work_ref[:, pl.ds(k, 1), :]
        pivot = jnp.sum(jnp.where(lane_row == k, row, 0.0), axis=2, keepdims=True)
        row = row / pivot
        column = jnp.sum(jnp.where(lane == k, work, 0.0), axis=2, keepdims=True)
        work_ref[...] = jnp.where(row_at == k, row, work - column * row)
        return carry

    lax.fori_loop(0, order, eliminate, 0)
    out_ref[...] = work_ref[:, :, order:]


def invert_spd(matrix):
    order = matrix.shape[1]
    symmetric = 0.5 * (matrix + jnp.swapaxes(matrix, 1, 2))
    eye = jnp.broadcast_to(jnp.eye(order, dtype=jnp.float32), matrix.shape)
    system = jnp.concatenate([symmetric, eye], axis=2)
    return pl.pallas_call(
        inverse_kernel,
        out_shape=jax.ShapeDtypeStruct(matrix.shape, jnp.float32),
        in_specs=[pl.BlockSpec(memory_space=pltpu.VMEM)],
        out_specs=pl.BlockSpec(memory_space=pltpu.VMEM),
        scratch_shapes=[pltpu.VMEM(system.shape, jnp.float32)],
        cost_estimate=pl.CostEstimate(
            flops=4 * system.size * order, bytes_accessed=system.size * 6,
            transcendentals=0),
    )(system)


def doubling_gather(block, axis, count):
    bits = count.bit_length() - 1
    spread = [0]
    first = None
    for bit in reversed(range(bits)):
        mask = 1 << bit
        other = lax.ppermute(block, axis, [(i, i ^ mask) for i in range(count)])
        first = other if first is None else first
        spread = spread + [s ^ mask for s in spread]
        if bit == 0:
            return block, other, spread, first
        block = jnp.concatenate([block, other], axis=0)


def first_match(mapping, targets):
    hit = mapping[:, :, None] == targets[None, None, :]
    index = jnp.argmax(hit, axis=1).astype(jnp.int32)
    return jnp.where(jnp.any(hit, axis=1), index, -1)


def per_device(diag_blocks, panel_rows, child_map, front):
    width = panel_rows.shape[1]
    row_index = lax.axis_index("prow")
    col_index = lax.axis_index("pcol")
    col_count = lax.axis_size("pcol")
    row_blocks = front.shape[0] // width
    col_blocks = front.shape[1] // width

    row_count = lax.axis_size("prow")

    local = jnp.transpose(panel_rows, (2, 0, 1)).reshape(width, 2 * width)
    near, far, spread, first = doubling_gather(local[None], "pcol", col_count)
    first, diag_blocks = lax.optimization_barrier((first, diag_blocks))
    half = near.shape[0]
    child_at = jnp.bitwise_xor(col_index, jnp.asarray(spread, jnp.int32))
    slot_of = jnp.bitwise_xor(col_index, jnp.arange(col_count, dtype=jnp.int32))
    slot_of = jnp.take(jnp.asarray(np.argsort(spread), jnp.int32), slot_of)

    pieces = [diag_blocks] + [
        lax.ppermute(diag_blocks, "prow", [(i, (i + k) % row_count) for i in range(row_count)])
        for k in range(1, row_count)
    ]
    order = (row_index - jnp.arange(row_count, dtype=jnp.int32)) % row_count
    whole_diag = sum(
        jnp.where((order == k)[None, :, None, None], piece[:, None], 0.0)
        for k, piece in enumerate(pieces)
    ).reshape(diag_blocks.shape[0], -1, diag_blocks.shape[2])

    first_col = col_index * col_blocks
    source = first_col // row_blocks
    source_map = lax.dynamic_slice_in_dim(child_map, source * col_count, col_count, 1)
    picks = first_match(source_map, first_col + jnp.arange(col_blocks, dtype=jnp.int32))
    keep = (picks >= 0) & (row_index == source)
    select = (picks[:, :, None] == child_at) & keep[:, :, None]
    select = select.astype(jnp.float32)
    window = sum(
        jnp.einsum("pjk,kbpa->pjba", select[:, :, part * half:(part + 1) * half],
                   held.reshape(half, width, 2, width), precision=HIGHEST)
        for part, held in enumerate((near, far))
    )
    window, whole_diag, child_map = lax.optimization_barrier((window, whole_diag, child_map))
    inverse = invert_spd(whole_diag)
    own_map = lax.dynamic_slice_in_dim(child_map, row_index * col_count, col_count, 1)
    table = first_match(own_map - row_index * row_blocks,
                        jnp.arange(row_blocks, dtype=jnp.int32))
    table = jnp.where(table >= 0, jnp.take(slot_of, jnp.maximum(table, 0)), -1)

    owner = [(c * col_blocks) // row_blocks for c in range(col_count)]
    def send(value, k):
        return lax.ppermute(value, ("prow", "pcol"), [
            (owner[c] * col_count + c, (owner[c] + k) * col_count + c)
            for c in range(col_count) if owner[c] + k < row_count
        ])

    nearest = jnp.stack([send(window[panel], 1) for panel in range(window.shape[0])])
    window = window + nearest + sum(send(window, k) for k in range(2, row_count))
    right = jnp.einsum("pxa,pjba->pxjb", inverse, window, precision=HIGHEST)
    right = right.reshape(2 * width, col_blocks * width)

    place = jnp.stack([row_index, col_index]).astype(jnp.int32)
    return apply_update(table, place, near, far, right, front, width, row_blocks, col_blocks)


def solution(mesh):
    return jax.shard_map(
        per_device,
        mesh=mesh,
        in_specs=(P(None, "prow", None), P(None, None, ("prow", "pcol")), P(), P("prow", "pcol")),
        out_specs=P("prow", "pcol"),
        check_vma=False,
    )
```

```python
import functools

import jax
import numpy as np
import jax.numpy as jnp
from jax import lax
from jax.experimental import pallas as pl
from jax.experimental.pallas import tpu as pltpu
from jax.sharding import PartitionSpec as P

HIGHEST = lax.Precision.HIGHEST
TILE_ROWS = 2048


def split_bf16(value):
    scaled = value * 65537.0
    high = scaled - (scaled - value)
    return high.astype(jnp.bfloat16), (value - high).astype(jnp.bfloat16)


def front_kernel(width, row_blocks, col_blocks, table_ref, place_ref,
                 near_ref, far_ref, stack_ref, front_ref, out_ref, left_ref):
    step = pl.program_id(0)
    tile_rows, cols = front_ref.shape
    per_tile = tile_rows // width
    half = near_ref.shape[0]

    def held(slot):
        near = near_ref[jnp.clip(slot, 0, half - 1)]
        far = far_ref[jnp.clip(slot - half, 0, half - 1)]
        return jnp.where(slot < half, near, far)

    first_row = place_ref[0] * row_blocks + step * per_tile
    first_col = place_ref[1] * col_blocks

    def update():
        lane = lax.broadcasted_iota(jnp.int32, (width, 2 * width), 1)
        for local in range(per_tile):
            block = step * per_tile + local
            first = table_ref[0, block]
            second = table_ref[1, block]
            from_first = held(first)
            from_second = held(second)
            left_ref[local * width:(local + 1) * width, :] = jnp.where(
                lane < width,
                jnp.where(first >= 0, from_first, 0.0),
                jnp.where(second >= 0, from_second, 0.0),
            )
        high, low = split_bf16(left_ref[...])
        return jnp.dot(jnp.concatenate([high, high, low], axis=1), stack_ref[...],
                       preferred_element_type=jnp.float32)

    all_upper = first_row + per_tile <= first_col
    all_lower = first_row >= first_col + col_blocks - 1

    @pl.when(all_upper)
    def _():
        out_ref[...] = front_ref[...]

    @pl.when(all_lower)
    def _():
        out_ref[...] = front_ref[...] - update()

    @pl.when(jnp.logical_not(all_upper | all_lower))
    def _():
        rows = first_row * width + lax.broadcasted_iota(jnp.int32, (tile_rows, cols), 0)
        cols_at = first_col * width + lax.broadcasted_iota(jnp.int32, (tile_rows, cols), 1)
        lower = rows >= jnp.bitwise_and(cols_at, -width)
        out_ref[...] = front_ref[...] - jnp.where(lower, update(), 0.0)


def apply_update(table, place, near, far, right, front, width, row_blocks, col_blocks):
    rows, cols = front.shape
    high, low = split_bf16(right)
    stack = jnp.concatenate([high, low, high], axis=0)
    tiles = rows // TILE_ROWS
    kernel = functools.partial(front_kernel, width, row_blocks, col_blocks)
    return pl.pallas_call(
        kernel,
        out_shape=jax.ShapeDtypeStruct(front.shape, front.dtype),
        grid_spec=pltpu.PrefetchScalarGridSpec(
            num_scalar_prefetch=2,
            grid=(tiles,),
            in_specs=[
                pl.BlockSpec(near.shape, lambda i, t, p: (0, 0, 0)),
                pl.BlockSpec(far.shape, lambda i, t, p: (0, 0, 0)),
                pl.BlockSpec(stack.shape, lambda i, t, p: (0, 0)),
                pl.BlockSpec((TILE_ROWS, cols), lambda i, t, p: (i, 0)),
            ],
            out_specs=pl.BlockSpec((TILE_ROWS, cols), lambda i, t, p: (i, 0)),
            scratch_shapes=[pltpu.VMEM((TILE_ROWS, 2 * width), jnp.float32)],
        ),
        cost_estimate=pl.CostEstimate(
            flops=3 * 2 * rows * cols * 2 * width,
            bytes_accessed=2 * rows * cols * 4 + 2 * near.size * 4 + stack.size * 2,
            transcendentals=0,
        ),
    )(table, place, near, far, stack, front)


def inverse_kernel(system_ref, out_ref, work_ref):
    order = out_ref.shape[1]
    shape = system_ref.shape
    lane = lax.broadcasted_iota(jnp.int32, shape, 2)
    lane_row = lax.broadcasted_iota(jnp.int32, (shape[0], 1, shape[2]), 2)
    row_at = lax.broadcasted_iota(jnp.int32, shape, 1)
    work_ref[...] = system_ref[...]

    def eliminate(k, carry):
        work = work_ref[...]
        row = work_ref[:, pl.ds(k, 1), :]
        pivot = jnp.sum(jnp.where(lane_row == k, row, 0.0), axis=2, keepdims=True)
        row = row / pivot
        column = jnp.sum(jnp.where(lane == k, work, 0.0), axis=2, keepdims=True)
        work_ref[...] = jnp.where(row_at == k, row, work - column * row)
        return carry

    lax.fori_loop(0, order, eliminate, 0)
    out_ref[...] = work_ref[:, :, order:]


def invert_spd(matrix):
    order = matrix.shape[1]
    symmetric = 0.5 * (matrix + jnp.swapaxes(matrix, 1, 2))
    eye = jnp.broadcast_to(jnp.eye(order, dtype=jnp.float32), matrix.shape)
    system = jnp.concatenate([symmetric, eye], axis=2)
    return pl.pallas_call(
        inverse_kernel,
        out_shape=jax.ShapeDtypeStruct(matrix.shape, jnp.float32),
        in_specs=[pl.BlockSpec(memory_space=pltpu.VMEM)],
        out_specs=pl.BlockSpec(memory_space=pltpu.VMEM),
        scratch_shapes=[pltpu.VMEM(system.shape, jnp.float32)],
        cost_estimate=pl.CostEstimate(
            flops=4 * system.size * order, bytes_accessed=system.size * 6,
            transcendentals=0),
    )(system)


def doubling_gather(block, axis, count):
    bits = count.bit_length() - 1
    spread = [0]
    first = None
    for bit in reversed(range(bits)):
        mask = 1 << bit
        other = lax.ppermute(block, axis, [(i, i ^ mask) for i in range(count)])
        first = other if first is None else first
        spread = spread + [s ^ mask for s in spread]
        if bit == 0:
            return block, other, spread, first
        block = jnp.concatenate([block, other], axis=0)


def first_match(mapping, targets):
    hit = mapping[:, :, None] == targets[None, None, :]
    index = jnp.argmax(hit, axis=1).astype(jnp.int32)
    return jnp.where(jnp.any(hit, axis=1), index, -1)


def per_device(diag_blocks, panel_rows, child_map, front):
    width = panel_rows.shape[1]
    row_index = lax.axis_index("prow")
    col_index = lax.axis_index("pcol")
    col_count = lax.axis_size("pcol")
    row_blocks = front.shape[0] // width
    col_blocks = front.shape[1] // width

    row_count = lax.axis_size("prow")

    local = jnp.transpose(panel_rows, (2, 0, 1)).reshape(width, 2 * width)
    near, far, spread, first = doubling_gather(local[None], "pcol", col_count)
    first, diag_blocks = lax.optimization_barrier((first, diag_blocks))
    half = near.shape[0]
    child_at = jnp.bitwise_xor(col_index, jnp.asarray(spread, jnp.int32))
    slot_of = jnp.bitwise_xor(col_index, jnp.arange(col_count, dtype=jnp.int32))
    slot_of = jnp.take(jnp.asarray(np.argsort(spread), jnp.int32), slot_of)

    pieces = [diag_blocks] + [
        lax.ppermute(diag_blocks, "prow", [(i, (i + k) % row_count) for i in range(row_count)])
        for k in range(1, row_count)
    ]
    order = (row_index - jnp.arange(row_count, dtype=jnp.int32)) % row_count
    whole_diag = sum(
        jnp.where((order == k)[None, :, None, None], piece[:, None], 0.0)
        for k, piece in enumerate(pieces)
    ).reshape(diag_blocks.shape[0], -1, diag_blocks.shape[2])

    first_col = col_index * col_blocks
    source = first_col // row_blocks
    source_map = lax.dynamic_slice_in_dim(child_map, source * col_count, col_count, 1)
    picks = first_match(source_map, first_col + jnp.arange(col_blocks, dtype=jnp.int32))
    keep = (picks >= 0) & (row_index == source)
    select = (picks[:, :, None] == child_at) & keep[:, :, None]
    select = select.astype(jnp.float32)
    window = sum(
        jnp.einsum("pjk,kbpa->pjba", select[:, :, part * half:(part + 1) * half],
                   held.reshape(half, width, 2, width), precision=HIGHEST)
        for part, held in enumerate((near, far))
    )
    window, whole_diag, child_map = lax.optimization_barrier((window, whole_diag, child_map))
    inverse = invert_spd(whole_diag)
    own_map = lax.dynamic_slice_in_dim(child_map, row_index * col_count, col_count, 1)
    table = first_match(own_map - row_index * row_blocks,
                        jnp.arange(row_blocks, dtype=jnp.int32))
    table = jnp.where(table >= 0, jnp.take(slot_of, jnp.maximum(table, 0)), -1)

    owner = [(c * col_blocks) // row_blocks for c in range(col_count)]
    def send(value, k):
        return lax.ppermute(value, ("prow", "pcol"), [
            (owner[c] * col_count + c, (owner[c] + k) * col_count + c)
            for c in range(col_count) if owner[c] + k < row_count
        ])

    nearest = jnp.stack([send(window[panel], 1) for panel in range(window.shape[0])])
    window = window + nearest + sum(send(window, k) for k in range(2, row_count))
    right = jnp.einsum("pxa,pjba->pxjb", inverse, window, precision=HIGHEST)
    right = right.reshape(2 * width, col_blocks * width)

    place = jnp.stack([row_index, col_index]).astype(jnp.int32)
    return apply_update(table, place, near, far, right, front, width, row_blocks, col_blocks)


def solution(mesh):
    return jax.shard_map(
        per_device,
        mesh=mesh,
        in_specs=(P(None, "prow", None), P(None, None, ("prow", "pcol")), P(), P("prow", "pcol")),
        out_specs=P("prow", "pcol"),
        check_vma=False,
    )
```

```python
import functools

import jax
import numpy as np
import jax.numpy as jnp
from jax import lax
from jax.experimental import pallas as pl
from jax.experimental.pallas import tpu as pltpu
from jax.sharding import PartitionSpec as P

HIGHEST = lax.Precision.HIGHEST
TILE_ROWS = 2048


def split_bf16(value):
    scaled = value * 65537.0
    high = scaled - (scaled - value)
    return high.astype(jnp.bfloat16), (value - high).astype(jnp.bfloat16)


def front_kernel(width, row_blocks, col_blocks, table_ref, place_ref,
                 near_ref, far_ref, stack_ref, front_ref, out_ref, left_ref):
    step = pl.program_id(0)
    tile_rows, cols = front_ref.shape
    per_tile = tile_rows // width
    half = near_ref.shape[0]

    def held(slot):
        near = near_ref[jnp.clip(slot, 0, half - 1)]
        far = far_ref[jnp.clip(slot - half, 0, half - 1)]
        return jnp.where(slot < half, near, far)

    first_row = place_ref[0] * row_blocks + step * per_tile
    first_col = place_ref[1] * col_blocks

    def update():
        lane = lax.broadcasted_iota(jnp.int32, (width, 2 * width), 1)
        for local in range(per_tile):
            block = step * per_tile + local
            first = table_ref[0, block]
            second = table_ref[1, block]
            from_first = held(first)
            from_second = held(second)
            left_ref[local * width:(local + 1) * width, :] = jnp.where(
                lane < width,
                jnp.where(first >= 0, from_first, 0.0),
                jnp.where(second >= 0, from_second, 0.0),
            )
        high, low = split_bf16(left_ref[...])
        return jnp.dot(jnp.concatenate([high, high, low], axis=1), stack_ref[...],
                       preferred_element_type=jnp.float32)

    all_upper = first_row + per_tile <= first_col
    all_lower = first_row >= first_col + col_blocks - 1

    @pl.when(all_upper)
    def _():
        out_ref[...] = front_ref[...]

    @pl.when(all_lower)
    def _():
        out_ref[...] = front_ref[...] - update()

    @pl.when(jnp.logical_not(all_upper | all_lower))
    def _():
        rows = first_row * width + lax.broadcasted_iota(jnp.int32, (tile_rows, cols), 0)
        cols_at = first_col * width + lax.broadcasted_iota(jnp.int32, (tile_rows, cols), 1)
        lower = rows >= jnp.bitwise_and(cols_at, -width)
        out_ref[...] = front_ref[...] - jnp.where(lower, update(), 0.0)


def apply_update(table, place, near, far, right, front, width, row_blocks, col_blocks):
    rows, cols = front.shape
    high, low = split_bf16(right)
    stack = jnp.concatenate([high, low, high], axis=0)
    tiles = rows // TILE_ROWS
    kernel = functools.partial(front_kernel, width, row_blocks, col_blocks)
    return pl.pallas_call(
        kernel,
        out_shape=jax.ShapeDtypeStruct(front.shape, front.dtype),
        grid_spec=pltpu.PrefetchScalarGridSpec(
            num_scalar_prefetch=2,
            grid=(tiles,),
            in_specs=[
                pl.BlockSpec(near.shape, lambda i, t, p: (0, 0, 0)),
                pl.BlockSpec(far.shape, lambda i, t, p: (0, 0, 0)),
                pl.BlockSpec(stack.shape, lambda i, t, p: (0, 0)),
                pl.BlockSpec((TILE_ROWS, cols), lambda i, t, p: (i, 0)),
            ],
            out_specs=pl.BlockSpec((TILE_ROWS, cols), lambda i, t, p: (i, 0)),
            scratch_shapes=[pltpu.VMEM((TILE_ROWS, 2 * width), jnp.float32)],
        ),
        cost_estimate=pl.CostEstimate(
            flops=3 * 2 * rows * cols * 2 * width,
            bytes_accessed=2 * rows * cols * 4 + 2 * near.size * 4 + stack.size * 2,
            transcendentals=0,
        ),
    )(table, place, near, far, stack, front)


def inverse_kernel(system_ref, out_ref, work_ref):
    order = out_ref.shape[1]
    shape = system_ref.shape
    lane = lax.broadcasted_iota(jnp.int32, shape, 2)
    lane_row = lax.broadcasted_iota(jnp.int32, (shape[0], 1, shape[2]), 2)
    row_at = lax.broadcasted_iota(jnp.int32, shape, 1)
    work_ref[...] = system_ref[...]

    def eliminate(k, carry):
        work = work_ref[...]
        row = work_ref[:, pl.ds(k, 1), :]
        pivot = jnp.sum(jnp.where(lane_row == k, row, 0.0), axis=2, keepdims=True)
        row = row / pivot
        column = jnp.sum(jnp.where(lane == k, work, 0.0), axis=2, keepdims=True)
        work_ref[...] = jnp.where(row_at == k, row, work - column * row)
        return carry

    lax.fori_loop(0, order, eliminate, 0)
    out_ref[...] = work_ref[:, :, order:]


def invert_spd(matrix):
    order = matrix.shape[1]
    symmetric = 0.5 * (matrix + jnp.swapaxes(matrix, 1, 2))
    eye = jnp.broadcast_to(jnp.eye(order, dtype=jnp.float32), matrix.shape)
    system = jnp.concatenate([symmetric, eye], axis=2)
    return pl.pallas_call(
        inverse_kernel,
        out_shape=jax.ShapeDtypeStruct(matrix.shape, jnp.float32),
        in_specs=[pl.BlockSpec(memory_space=pltpu.VMEM)],
        out_specs=pl.BlockSpec(memory_space=pltpu.VMEM),
        scratch_shapes=[pltpu.VMEM(system.shape, jnp.float32)],
        cost_estimate=pl.CostEstimate(
            flops=4 * system.size * order, bytes_accessed=system.size * 6,
            transcendentals=0),
    )(system)


def doubling_gather(block, axis, count):
    bits = count.bit_length() - 1
    spread = [0]
    first = None
    for bit in reversed(range(bits)):
        mask = 1 << bit
        other = lax.ppermute(block, axis, [(i, i ^ mask) for i in range(count)])
        first = other if first is None else first
        spread = spread + [s ^ mask for s in spread]
        if bit == 0:
            return block, other, spread, first
        block = jnp.concatenate([block, other], axis=0)


def first_match(mapping, targets):
    hit = mapping[:, :, None] == targets[None, None, :]
    index = jnp.argmax(hit, axis=1).astype(jnp.int32)
    return jnp.where(jnp.any(hit, axis=1), index, -1)


def per_device(diag_blocks, panel_rows, child_map, front):
    width = panel_rows.shape[1]
    row_index = lax.axis_index("prow")
    col_index = lax.axis_index("pcol")
    col_count = lax.axis_size("pcol")
    row_blocks = front.shape[0] // width
    col_blocks = front.shape[1] // width

    row_count = lax.axis_size("prow")

    local = jnp.transpose(panel_rows, (2, 0, 1)).reshape(width, 2 * width)
    near, far, spread, first = doubling_gather(local[None], "pcol", col_count)
    first, diag_blocks = lax.optimization_barrier((first, diag_blocks))
    half = near.shape[0]
    child_at = jnp.bitwise_xor(col_index, jnp.asarray(spread, jnp.int32))
    slot_of = jnp.bitwise_xor(col_index, jnp.arange(col_count, dtype=jnp.int32))
    slot_of = jnp.take(jnp.asarray(np.argsort(spread), jnp.int32), slot_of)

    pieces = [diag_blocks] + [
        lax.ppermute(diag_blocks, "prow", [(i, (i + k) % row_count) for i in range(row_count)])
        for k in range(1, row_count)
    ]
    order = (row_index - jnp.arange(row_count, dtype=jnp.int32)) % row_count
    whole_diag = sum(
        jnp.where((order == k)[None, :, None, None], piece[:, None], 0.0)
        for k, piece in enumerate(pieces)
    ).reshape(diag_blocks.shape[0], -1, diag_blocks.shape[2])

    first_col = col_index * col_blocks
    source = first_col // row_blocks
    source_map = lax.dynamic_slice_in_dim(child_map, source * col_count, col_count, 1)
    picks = first_match(source_map, first_col + jnp.arange(col_blocks, dtype=jnp.int32))
    keep = (picks >= 0) & (row_index == source)
    select = (picks[:, :, None] == child_at) & keep[:, :, None]
    select = select.astype(jnp.float32)
    window = sum(
        jnp.einsum("pjk,kbpa->pjba", select[:, :, part * half:(part + 1) * half],
                   held.reshape(half, width, 2, width), precision=HIGHEST)
        for part, held in enumerate((near, far))
    )
    window, whole_diag, child_map = lax.optimization_barrier((window, whole_diag, child_map))
    inverse = invert_spd(whole_diag)
    own_map = lax.dynamic_slice_in_dim(child_map, row_index * col_count, col_count, 1)
    table = first_match(own_map - row_index * row_blocks,
                        jnp.arange(row_blocks, dtype=jnp.int32))
    table = jnp.where(table >= 0, jnp.take(slot_of, jnp.maximum(table, 0)), -1)

    owner = [(c * col_blocks) // row_blocks for c in range(col_count)]
    def send(value, k):
        return lax.ppermute(value, ("prow", "pcol"), [
            (owner[c] * col_count + c, (owner[c] + k) * col_count + c)
            for c in range(col_count) if owner[c] + k < row_count
        ])

    window = window + sum(
        jnp.stack([send(window[panel], k) for panel in range(window.shape[0])])
        for k in range(1, row_count)
    )
    right = jnp.einsum("pxa,pjba->pxjb", inverse, window, precision=HIGHEST)
    right = right.reshape(2 * width, col_blocks * width)

    place = jnp.stack([row_index, col_index]).astype(jnp.int32)
    return apply_update(table, place, near, far, right, front, width, row_blocks, col_blocks)


def solution(mesh):
    return jax.shard_map(
        per_device,
        mesh=mesh,
        in_specs=(P(None, "prow", None), P(None, None, ("prow", "pcol")), P(), P("prow", "pcol")),
        out_specs=P("prow", "pcol"),
        check_vma=False,
    )
```

```python
import functools

import jax
import numpy as np
import jax.numpy as jnp
from jax import lax
from jax.experimental import pallas as pl
from jax.experimental.pallas import tpu as pltpu
from jax.sharding import PartitionSpec as P

HIGHEST = lax.Precision.HIGHEST
TILE_ROWS = 4096


def split_bf16(value):
    scaled = value * 65537.0
    high = scaled - (scaled - value)
    return high.astype(jnp.bfloat16), (value - high).astype(jnp.bfloat16)


def front_kernel(width, row_blocks, col_blocks, table_ref, place_ref,
                 near_ref, far_ref, stack_ref, front_ref, out_ref, left_ref):
    step = pl.program_id(0)
    tile_rows, cols = front_ref.shape
    per_tile = tile_rows // width
    half = near_ref.shape[0]

    def held(slot):
        near = near_ref[jnp.clip(slot, 0, half - 1)]
        far = far_ref[jnp.clip(slot - half, 0, half - 1)]
        return jnp.where(slot < half, near, far)

    first_row = place_ref[0] * row_blocks + step * per_tile
    first_col = place_ref[1] * col_blocks

    def update():
        lane = lax.broadcasted_iota(jnp.int32, (width, 2 * width), 1)
        for local in range(per_tile):
            block = step * per_tile + local
            first = table_ref[0, block]
            second = table_ref[1, block]
            from_first = held(first)
            from_second = held(second)
            left_ref[local * width:(local + 1) * width, :] = jnp.where(
                lane < width,
                jnp.where(first >= 0, from_first, 0.0),
                jnp.where(second >= 0, from_second, 0.0),
            )
        high, low = split_bf16(left_ref[...])
        return jnp.dot(jnp.concatenate([high, high, low], axis=1), stack_ref[...],
                       preferred_element_type=jnp.float32)

    all_upper = first_row + per_tile <= first_col
    all_lower = first_row >= first_col + col_blocks - 1

    @pl.when(all_upper)
    def _():
        out_ref[...] = front_ref[...]

    @pl.when(all_lower)
    def _():
        out_ref[...] = front_ref[...] - update()

    @pl.when(jnp.logical_not(all_upper | all_lower))
    def _():
        rows = first_row * width + lax.broadcasted_iota(jnp.int32, (tile_rows, cols), 0)
        cols_at = first_col * width + lax.broadcasted_iota(jnp.int32, (tile_rows, cols), 1)
        lower = rows >= jnp.bitwise_and(cols_at, -width)
        out_ref[...] = front_ref[...] - jnp.where(lower, update(), 0.0)


def apply_update(table, place, near, far, right, front, width, row_blocks, col_blocks):
    rows, cols = front.shape
    high, low = split_bf16(right)
    stack = jnp.concatenate([high, low, high], axis=0)
    tiles = rows // TILE_ROWS
    kernel = functools.partial(front_kernel, width, row_blocks, col_blocks)
    return pl.pallas_call(
        kernel,
        out_shape=jax.ShapeDtypeStruct(front.shape, front.dtype),
        grid_spec=pltpu.PrefetchScalarGridSpec(
            num_scalar_prefetch=2,
            grid=(tiles,),
            in_specs=[
                pl.BlockSpec(near.shape, lambda i, t, p: (0, 0, 0)),
                pl.BlockSpec(far.shape, lambda i, t, p: (0, 0, 0)),
                pl.BlockSpec(stack.shape, lambda i, t, p: (0, 0)),
                pl.BlockSpec((TILE_ROWS, cols), lambda i, t, p: (i, 0)),
            ],
            out_specs=pl.BlockSpec((TILE_ROWS, cols), lambda i, t, p: (i, 0)),
            scratch_shapes=[pltpu.VMEM((TILE_ROWS, 2 * width), jnp.float32)],
        ),
        cost_estimate=pl.CostEstimate(
            flops=3 * 2 * rows * cols * 2 * width,
            bytes_accessed=2 * rows * cols * 4 + 2 * near.size * 4 + stack.size * 2,
            transcendentals=0,
        ),
    )(table, place, near, far, stack, front)


def inverse_kernel(system_ref, out_ref, work_ref):
    order = out_ref.shape[1]
    shape = system_ref.shape
    lane = lax.broadcasted_iota(jnp.int32, shape, 2)
    lane_row = lax.broadcasted_iota(jnp.int32, (shape[0], 1, shape[2]), 2)
    row_at = lax.broadcasted_iota(jnp.int32, shape, 1)
    work_ref[...] = system_ref[...]

    def eliminate(k, carry):
        work = work_ref[...]
        row = work_ref[:, pl.ds(k, 1), :]
        pivot = jnp.sum(jnp.where(lane_row == k, row, 0.0), axis=2, keepdims=True)
        row = row / pivot
        column = jnp.sum(jnp.where(lane == k, work, 0.0), axis=2, keepdims=True)
        work_ref[...] = jnp.where(row_at == k, row, work - column * row)
        return carry

    lax.fori_loop(0, order, eliminate, 0)
    out_ref[...] = work_ref[:, :, order:]


def invert_spd(matrix):
    order = matrix.shape[1]
    symmetric = 0.5 * (matrix + jnp.swapaxes(matrix, 1, 2))
    eye = jnp.broadcast_to(jnp.eye(order, dtype=jnp.float32), matrix.shape)
    system = jnp.concatenate([symmetric, eye], axis=2)
    return pl.pallas_call(
        inverse_kernel,
        out_shape=jax.ShapeDtypeStruct(matrix.shape, jnp.float32),
        in_specs=[pl.BlockSpec(memory_space=pltpu.VMEM)],
        out_specs=pl.BlockSpec(memory_space=pltpu.VMEM),
        scratch_shapes=[pltpu.VMEM(system.shape, jnp.float32)],
        cost_estimate=pl.CostEstimate(
            flops=4 * system.size * order, bytes_accessed=system.size * 6,
            transcendentals=0),
    )(system)


def doubling_gather(block, axis, count):
    bits = count.bit_length() - 1
    spread = [0]
    first = None
    for bit in reversed(range(bits)):
        mask = 1 << bit
        other = lax.ppermute(block, axis, [(i, i ^ mask) for i in range(count)])
        first = other if first is None else first
        spread = spread + [s ^ mask for s in spread]
        if bit == 0:
            return block, other, spread, first
        block = jnp.concatenate([block, other], axis=0)


def first_match(mapping, targets):
    hit = mapping[:, :, None] == targets[None, None, :]
    index = jnp.argmax(hit, axis=1).astype(jnp.int32)
    return jnp.where(jnp.any(hit, axis=1), index, -1)


def per_device(diag_blocks, panel_rows, child_map, front):
    width = panel_rows.shape[1]
    row_index = lax.axis_index("prow")
    col_index = lax.axis_index("pcol")
    col_count = lax.axis_size("pcol")
    row_blocks = front.shape[0] // width
    col_blocks = front.shape[1] // width

    row_count = lax.axis_size("prow")

    local = jnp.transpose(panel_rows, (2, 0, 1)).reshape(width, 2 * width)
    near, far, spread, first = doubling_gather(local[None], "pcol", col_count)
    first, diag_blocks = lax.optimization_barrier((first, diag_blocks))
    half = near.shape[0]
    child_at = jnp.bitwise_xor(col_index, jnp.asarray(spread, jnp.int32))
    slot_of = jnp.bitwise_xor(col_index, jnp.arange(col_count, dtype=jnp.int32))
    slot_of = jnp.take(jnp.asarray(np.argsort(spread), jnp.int32), slot_of)

    pieces = [diag_blocks] + [
        lax.ppermute(diag_blocks, "prow", [(i, (i + k) % row_count) for i in range(row_count)])
        for k in range(1, row_count)
    ]
    order = (row_index - jnp.arange(row_count, dtype=jnp.int32)) % row_count
    whole_diag = sum(
        jnp.where((order == k)[None, :, None, None], piece[:, None], 0.0)
        for k, piece in enumerate(pieces)
    ).reshape(diag_blocks.shape[0], -1, diag_blocks.shape[2])

    first_col = col_index * col_blocks
    source = first_col // row_blocks
    source_map = lax.dynamic_slice_in_dim(child_map, source * col_count, col_count, 1)
    picks = first_match(source_map, first_col + jnp.arange(col_blocks, dtype=jnp.int32))
    keep = (picks >= 0) & (row_index == source)
    select = (picks[:, :, None] == child_at) & keep[:, :, None]
    select = select.astype(jnp.float32)
    window = sum(
        jnp.einsum("pjk,kbpa->pjba", select[:, :, part * half:(part + 1) * half],
                   held.reshape(half, width, 2, width), precision=HIGHEST)
        for part, held in enumerate((near, far))
    )
    window, whole_diag, child_map = lax.optimization_barrier((window, whole_diag, child_map))
    inverse = invert_spd(whole_diag)
    own_map = lax.dynamic_slice_in_dim(child_map, row_index * col_count, col_count, 1)
    table = first_match(own_map - row_index * row_blocks,
                        jnp.arange(row_blocks, dtype=jnp.int32))
    table = jnp.where(table >= 0, jnp.take(slot_of, jnp.maximum(table, 0)), -1)

    owner = [(c * col_blocks) // row_blocks for c in range(col_count)]
    def send(value, k):
        return lax.ppermute(value, ("prow", "pcol"), [
            (owner[c] * col_count + c, (owner[c] + k) * col_count + c)
            for c in range(col_count) if owner[c] + k < row_count
        ])

    nearest = jnp.stack([send(window[panel], 1) for panel in range(window.shape[0])])
    window = window + nearest + sum(send(window, k) for k in range(2, row_count))
    right = jnp.einsum("pxa,pjba->pxjb", inverse, window, precision=HIGHEST)
    right = right.reshape(2 * width, col_blocks * width)

    place = jnp.stack([row_index, col_index]).astype(jnp.int32)
    return apply_update(table, place, near, far, right, front, width, row_blocks, col_blocks)


def solution(mesh):
    return jax.shard_map(
        per_device,
        mesh=mesh,
        in_specs=(P(None, "prow", None), P(None, None, ("prow", "pcol")), P(), P("prow", "pcol")),
        out_specs=P("prow", "pcol"),
        check_vma=False,
    )
```
